512 devices in a mesh: blk: 16 (over x_lo, y), exp: 32 (over z, x_hi, core).
Axes of the slice: x: 4 (x_hi: 2, x_lo: 2; x = x_hi * 2 + x_lo), y: 8, z: 8, core: 2. Of those that a mesh axis runs over, the one named last changes fastest.
Arguments:
- residual: bfloat16 [32, 2048, 1024], P('exp', 'blk'), may hold values from -6 to 6
- queries: bfloat16 [32, 2048, 1024], P('exp', 'blk'), may hold values from -6 to 6
- suffix_kv: bfloat16 [32, 2048, 1024], P('exp', 'blk'), may hold values from -6 to 6
- prompt_kv: bfloat16 [32, 1024, 1024], P('exp', 'blk'), may hold values from -6 to 6
- prompt_lengths: int32 [32], P('exp'), may hold values from 1 to 1024, as said below
- block_keep: int32 [32, 32], P('exp', 'blk'), may hold values 0 or 1
- suffix_lengths: int32 [32, 16, 4], P('exp', 'blk'), may hold values from 1 to 64, 128 in all within a row
- out_weight: bfloat16 [1024, 1024], P('exp'), may hold values from -0.75 to 0.75
- routes: int32 [32, 2048, 8], P('exp', 'blk'), may hold values from 0 to 31, all different within a row; in each aligned block of 128 rows (0 to 127, 128 to 255, ..., all dimensions but the last counted through in order) at most 40 rows name the same one
- route_weight: float32 [32, 2048, 8], P('exp', 'blk'), may hold values from 0.02 to 0.25
- gate_up_weight: bfloat16 [32, 1024, 1024], P('exp'), may hold values from -0.1875 to 0.1875
- down_weight: bfloat16 [32, 512, 1024], P('exp'), may hold values from -0.25 to 0.25
- page_owner: int32 [32, 128, 1], P('exp', 'blk'), may hold values from 0 to 15; in each aligned block of 8 rows (0 to 7, 8 to 15, ..., all dimensions but the last counted through in order) at most 2 rows name the same one
Outputs:
- attended: bfloat16 [32, 2048, 1024], P('exp', 'blk')
- layer_out: bfloat16 [32, 2048, 1024], P('exp', 'blk')
- cache_pages: bfloat16 [32, 4096, 1024], P('exp', 'blk')
The draws below stay inside these ranges and needn't reach their ends.
Inputs may be any that keep to these rules, and one draw needn't show every extreme that they name: `prompt_lengths`: some group's prompt length equals 1024. `suffix_lengths`: each device's 4 request lengths sum to 128. `routes`: each token names 8 different experts; among the tokens of one device at most 40 name any one expert, and that bound is reached. `page_owner`: among the 8 pages of one device at most 2 go to any one owner, and that bound is reached.
All inputs are finite; a program needn't handle non-finite values. No bound on the sum of `block_keep` on one device may be relied on, other than what follows from the above.
Results may differ from the reference program's by a relative error of at most 0.013.
Values may be sent and summed in bfloat16 or wider, within the bound.
No kernel may reach another device: no remote copies, remote signals or barrier semaphores. Data moves between devices by JAX's collectives and lax.ppermute only.
A program may use at most 64 MiB of HBM per device.

```python
import math
import jax
import jax.numpy as jnp
import numpy as np
from jax import lax

D = 1024
H = 16
KVH = 8
HD = 64
FF = 512
TOPK = 8
EXPERTS = 32
TOK_DEV = 128
KB = 32
PAGE = 8
REQS = 4
SUF_MOST = 64
SUFFIX = 2048
PROMPT = 1024
CAP = 40
PAGES = 8
CAPP = 2
N_BLK = 16
N_EXP = 32


def draw_queries(key, part):
    shape = (N_EXP, SUFFIX, H * HD)
    values = jnp.clip(jax.random.normal(jax.random.fold_in(key, 1), shape, jnp.float32), -6.0, 6.0)
    return values.astype(jnp.bfloat16)


def draw_prompt_kv(key, part):
    shape = (N_EXP, PROMPT, 2 * KVH * HD)
    values = jnp.clip(jax.random.normal(jax.random.fold_in(key, 2), shape, jnp.float32), -6.0, 6.0)
    return values.astype(jnp.bfloat16)


def draw_prompt_lengths(key, part):
    drawn = jax.random.randint(jax.random.fold_in(key, 3), (N_EXP,), 1, PROMPT + 1)
    chosen = jax.random.randint(jax.random.fold_in(key, 4), (), 0, N_EXP)
    return jnp.where(jnp.arange(N_EXP, dtype=jnp.int32) == chosen, PROMPT, drawn).astype(jnp.int32)


def place_ends(values, key, low, largest):
    spot = [jax.random.randint(jax.random.fold_in(key, axis), (), 0, length) for axis, length in enumerate(values.shape)]
    widest = values.shape.index(max(values.shape))
    neighbour = spot[:widest] + [(spot[widest] + 1) % values.shape[widest]] + spot[widest + 1:]
    return values.at[tuple(spot)].set(low).at[tuple(neighbour)].set(largest)


def levels(rng, extent, shards, least, largest):
    factor_of, own = 1.0, jax.random.fold_in(rng, 6)
    for dim, blocks in shards:
        heights = jnp.exp(jax.random.uniform(jax.random.fold_in(own, dim), (blocks,), jnp.float32, least / len(shards), largest / len(shards)))
        factor_of = factor_of * jnp.repeat(heights, extent[dim] // blocks).reshape([-1 if axis == dim else 1 for axis in range(len(extent))])
    return factor_of


def split_up(count, total, most, skew):
    weights = [(1 << 20) // math.isqrt(rank ** skew) + 1 for rank in range(2, count + 1)]
    rest, counts = total - most - (count - 1), [1] * (count - 1)
    while rest > 0:
        candidates = [i for i in range(count - 1) if counts[i] < most]
        mass, budget = sum([weights[i] for i in candidates]), rest
        for i in candidates:
            addition = min(most - counts[i], max(1, budget * weights[i] // mass), rest)
            counts[i] = counts[i] + addition
            rest = rest - addition
    return np.array([most] + counts)


def uneven(rng, number_of, total, bound, slope):
    if number_of == 2:
        one = jax.random.randint(rng, (), max(1, total - bound), min(bound, total - 1) + 1)
        return jnp.stack([one, total - one])
    tallies = jnp.asarray(split_up(number_of, total, bound, slope), jnp.int32)
    twos = (number_of - 1) // 2
    donor, sink = tallies[1:1 + 2 * twos:2], tallies[2:2 + 2 * twos:2]
    room = jnp.minimum(donor - 1, bound - sink)
    shifted = jax.random.randint(jax.random.fold_in(rng, 1), (twos,), 0, 1 << 20) % (room + 1)
    tallies = tallies.at[1:1 + 2 * twos:2].set(donor - shifted).at[2:2 + 2 * twos:2].set(sink + shifted)
    return tallies[jax.random.permutation(jax.random.fold_in(rng, 2), number_of)]


def shared_out(rng, own, number, rows, count, top, bound, skew):
    sequence = jax.random.permutation(rng, count)
    packed, common = load_shares(count, rows * top, bound, skew, True), load_shares(count, rows * top, bound, skew, False)
    places = jnp.arange(count)

    def named(sizes, offset_by):
        used = int((sizes > 0).sum())
        fixed = max(1, used // 4)
        shifted = fixed + (places - fixed + offset_by * (used - fixed)) % max(1, count - fixed)
        return jnp.zeros((count,), jnp.int32).at[sequence[jnp.where(places < fixed, places, shifted)]].set(jnp.asarray(sizes, jnp.int32))

    sizes = jnp.where(number % 4 == 0, named(packed, number // 4), named(common, number - number // 4 - 1))
    mixed = jax.random.permutation(jax.random.fold_in(own, 3), count)
    donor, sink = mixed[0:count // 2 * 2:2], mixed[1:count // 2 * 2:2]
    slack = jnp.minimum(sizes[donor] - 1, bound - sizes[sink]) // 2
    slack = jnp.where((donor == sequence[0]) | (sink == sequence[0]) | (sizes[sink] == 0), 0, jnp.maximum(slack, 0))
    shifted = jax.random.randint(jax.random.fold_in(own, 4), (count // 2,), 0, 1 << 20) % (slack + 1)
    sizes = sizes.at[donor].add(-shifted).at[sink].add(shifted)
    items = jnp.searchsorted(jnp.cumsum(sizes), jnp.arange(rows * top), side="right").astype(jnp.int32)
    grid = items.reshape(top, rows).T
    grid = grid[jax.random.permutation(jax.random.fold_in(own, 1), rows)]
    offset_by = jax.random.randint(jax.random.fold_in(own, 2), (rows, 1), 0, top)
    return jnp.take_along_axis(grid, (jnp.arange(top)[None, :] + offset_by) % top, axis=1)


def load_shares(count, total, most, skew, full):
    loads = [(1 << 20) // math.isqrt(standing ** skew) + 1 for standing in range(1, count + 1)]
    largest = most if full else min(most, max(-(-total // count), total * loads[0] // sum(loads)))
    least = 1 if total - largest >= count - 1 else 0
    counts, surplus = [largest] + [least] * (count - 1), total - largest - least * (count - 1)
    while surplus > 0:
        free = [i for i in range(1, count) if counts[i] < largest] or [i for i in range(1, count) if counts[i] < most]
        mass, remaining = sum([loads[i] for i in free]), surplus
        for i in free:
            more = min(most - counts[i], max(1, remaining * loads[i] // mass), surplus)
            counts[i] = counts[i] + more
            surplus = surplus - more
    return np.array(counts)


def gaussian(rng, shape, scale, reach, pieces=(), kind=jnp.bfloat16):
    loudness = levels(rng, shape, pieces, -0.22, 0.18) if pieces else 1.0
    entries = jax.random.normal(rng, shape, jnp.float32) * scale * loudness
    return jnp.minimum(jnp.maximum(entries, -reach), reach).astype(kind)


def setup_inputs(seed: int = 0) -> dict:
    seeds = jax.random.split(jax.random.key(seed), 14)
    residual = gaussian(seeds[0], (N_EXP, SUFFIX, D), 1.0, 6.0, ((0, 32), (1, 16)))
    queries = draw_queries(jax.random.fold_in(seeds[13], 71), 0)
    suffix_kv = gaussian(seeds[2], (N_EXP, SUFFIX, 2 * KVH * HD), 1.0, 6.0, ((0, 32), (1, 16)))
    prompt_kv = draw_prompt_kv(jax.random.fold_in(seeds[13], 71), 0)
    prompt_lengths = draw_prompt_lengths(jax.random.fold_in(seeds[13], 71), 0)
    block_keep = place_ends((jax.random.randint(seeds[5], (N_EXP, PROMPT // KB), 0, 4) < 3).astype(jnp.int32), jax.random.fold_in(seeds[5], 1), 0, 1)
    suffix_lengths = jax.vmap(lambda own: uneven(own, REQS, TOK_DEV, SUF_MOST, 2))(jax.random.split(seeds[6], N_EXP * N_BLK)).reshape((N_EXP, N_BLK, REQS)).astype(jnp.int32)
    out_weight = gaussian(seeds[7], (H * HD, D), HD ** -0.5, 0.75, ((0, 32),))
    routes_keys = jax.random.split(jax.random.fold_in(seeds[8], 1), N_EXP * SUFFIX // TOK_DEV)
    routes_turns = jax.random.permutation(jax.random.fold_in(seeds[8], 3), N_EXP * SUFFIX // TOK_DEV)
    routes = jax.vmap(lambda own, number: shared_out(jax.random.fold_in(seeds[8], 2), own, number, TOK_DEV, EXPERTS, TOPK, CAP, 2))(routes_keys, routes_turns).reshape((N_EXP, SUFFIX, TOPK))
    route_weight = jnp.clip(0.02 + 0.23 * jax.random.uniform(seeds[9], (N_EXP, SUFFIX, TOPK), jnp.float32) ** levels(seeds[9], (N_EXP, SUFFIX, TOPK), ((0, 32), (1, 16)), -0.2, 0.2), 0.02, 0.25)
    gate_up_weight = gaussian(seeds[10], (EXPERTS, D, 2 * FF), D ** -0.5, 0.1875, ((0, 32),))
    down_weight = gaussian(seeds[11], (EXPERTS, FF, D), FF ** -0.5, 0.25, ((0, 32),))
    page_owner_keys = jax.random.split(jax.random.fold_in(seeds[12], 1), N_EXP * (PROMPT // PAGE) // PAGES)
    page_owner_turns = jax.random.permutation(jax.random.fold_in(seeds[12], 3), N_EXP * (PROMPT // PAGE) // PAGES)
    page_owner = jax.vmap(lambda own, number: shared_out(jax.random.fold_in(seeds[12], 2), own, number, PAGES, N_BLK, 1, CAPP, 1))(page_owner_keys, page_owner_turns).reshape((N_EXP, PROMPT // PAGE, 1))
    return {"residual": residual, "queries": queries, "suffix_kv": suffix_kv, "prompt_kv": prompt_kv, "prompt_lengths": prompt_lengths, "block_keep": block_keep, "suffix_lengths": suffix_lengths, "out_weight": out_weight, "routes": routes, "route_weight": route_weight, "gate_up_weight": gate_up_weight, "down_weight": down_weight, "page_owner": page_owner}


SCALE = 0.125
NEGATIVE = -1e+30
EPSILON = 1e-06

def segment_of(lengths, count):
    ends = jnp.cumsum(lengths).astype(jnp.int32)
    position = jnp.arange(count, dtype=jnp.int32)
    return lax.optimization_barrier(jnp.sum((position[:, None] >= ends[None, :]).astype(jnp.int32), axis=1))

def rank_within(labels, count):
    onehot = (labels[:, None] == jnp.arange(count, dtype=jnp.int32)[None, :]).astype(jnp.int32)
    before = jnp.cumsum(onehot, axis=0) - onehot
    return lax.optimization_barrier(jnp.sum(before * onehot, axis=1)).astype(jnp.int32)

def attend_device(query_rows, suffix_rows, prompt_rows, prompt_live, lengths):
    group_size = H // KVH
    kv_width = KVH * HD
    tok_rows = query_rows.shape[0]
    query_heads = query_rows.astype(jnp.float32).reshape(tok_rows, KVH, group_size, HD)
    key_heads = jnp.concatenate([prompt_rows[:, :kv_width], suffix_rows[:, :kv_width]], 0).astype(jnp.float32).reshape(-1, KVH, HD)
    value_heads = jnp.concatenate([prompt_rows[:, kv_width:], suffix_rows[:, kv_width:]], 0).astype(jnp.float32).reshape(-1, KVH, HD)
    scores = jnp.einsum('tkgd,skd->tkgs', query_heads, key_heads) * SCALE
    segment = segment_of(lengths, tok_rows)
    position = jnp.arange(tok_rows, dtype=jnp.int32)
    own_seen = (segment[:, None] == segment[None, :]) & (position[None, :] <= position[:, None])
    prompt_seen = jnp.broadcast_to(prompt_live[None, :], (tok_rows, prompt_live.shape[0]))
    visible = jnp.concatenate([prompt_seen, own_seen], 1)[:, None, None, :]
    peak = lax.optimization_barrier(jnp.max(jnp.where(visible, scores, NEGATIVE), axis=-1, keepdims=True))
    weight = jnp.where(visible, jnp.exp(scores - peak), 0.0)
    denom = lax.optimization_barrier(jnp.sum(weight, axis=-1))
    rounded = lax.optimization_barrier(weight.astype(jnp.bfloat16)).astype(jnp.float32)
    numerator = jnp.einsum('tkgs,skd->tkgd', rounded, value_heads)
    return (numerator / denom[..., None]).reshape(tok_rows, H * HD).astype(jnp.bfloat16)

def attention(queries, suffix_kv, prompt_kv, prompt_lengths, block_keep, suffix_lengths):

    def per_group(group_idx):
        prompt_live = (jnp.repeat(block_keep[group_idx], KB) > 0) & (jnp.arange(PROMPT, dtype=jnp.int32) < prompt_lengths[group_idx])
        group_queries = queries[group_idx].reshape(N_BLK, TOK_DEV, H * HD)
        group_suffix = suffix_kv[group_idx].reshape(N_BLK, TOK_DEV, 2 * KVH * HD)
        group_prompt = prompt_kv[group_idx]

        def per_device(blk_idx):
            return attend_device(group_queries[blk_idx], group_suffix[blk_idx], group_prompt, prompt_live, suffix_lengths[group_idx, blk_idx])
        return lax.map(per_device, jnp.arange(N_BLK, dtype=jnp.int32)).reshape(SUFFIX, H * HD)
    return lax.map(per_group, jnp.arange(N_EXP, dtype=jnp.int32))

def experts_row(normed, routes, weights, stream, gate_up_weight, down_weight):

    def dispatch_one(token_rows, token_routes):
        flat_routes = token_routes.reshape(-1)
        slot_index = flat_routes * CAP + rank_within(flat_routes, EXPERTS)
        buffer = jnp.zeros((EXPERTS * CAP, D), jnp.bfloat16).at[slot_index].set(jnp.repeat(token_rows, TOPK, axis=0))
        return (buffer.reshape(EXPERTS, CAP, D), slot_index)
    buffers, slots = jax.vmap(dispatch_one)(normed, routes)

    def run_expert(expert_idx):
        picked_rows = buffers[:, expert_idx].reshape(N_EXP * CAP, D)
        gate_up = jnp.dot(picked_rows, gate_up_weight[expert_idx], preferred_element_type=jnp.float32)
        hidden = (jax.nn.silu(gate_up[:, :FF]) * gate_up[:, FF:]).astype(jnp.bfloat16)
        result = jnp.dot(hidden, down_weight[expert_idx], preferred_element_type=jnp.float32).astype(jnp.bfloat16)
        return result.reshape(N_EXP, CAP, D)
    outputs = lax.map(run_expert, jnp.arange(EXPERTS, dtype=jnp.int32))
    returned = jnp.transpose(outputs, (1, 0, 2, 3)).reshape(N_EXP, EXPERTS * CAP, D)

    def combine(table, slot_index, route_w, stream_rows):
        picked = table[slot_index].astype(jnp.float32).reshape(TOK_DEV, TOPK, D)
        return (stream_rows.astype(jnp.float32) + lax.optimization_barrier(jnp.sum(picked * route_w[:, :, None], axis=1))).astype(jnp.bfloat16)
    return jax.vmap(combine)(returned, slots, weights, stream)

def regroup(prompt_rows, owner):
    page_rows = prompt_rows.reshape(N_BLK * PAGES, PAGE, prompt_rows.shape[-1])
    owners = owner[:, 0].reshape(N_BLK, PAGES)
    ranks = jax.vmap(lambda labels: rank_within(labels, N_BLK))(owners)
    source = jnp.arange(N_BLK, dtype=jnp.int32)[:, None]
    page_slot = ((owners * N_BLK + source) * CAPP + ranks).reshape(-1)
    result = jnp.zeros((N_BLK * N_BLK * CAPP, PAGE, prompt_rows.shape[-1]), prompt_rows.dtype).at[page_slot].set(page_rows)
    return result.reshape(N_BLK * N_BLK * CAPP * PAGE, prompt_rows.shape[-1])

def reference(residual, queries, suffix_kv, prompt_kv, prompt_lengths, block_keep, suffix_lengths, out_weight, routes, route_weight, gate_up_weight, down_weight, page_owner):
    attended = attention(queries, suffix_kv, prompt_kv, prompt_lengths, block_keep, suffix_lengths)
    projected = jnp.dot(attended.reshape(-1, H * HD), out_weight, preferred_element_type=jnp.float32)
    stream = (residual.reshape(-1, D).astype(jnp.float32) + projected).astype(jnp.bfloat16)
    stream_f32 = lax.optimization_barrier(stream).astype(jnp.float32)
    normed = (stream_f32 * lax.rsqrt(lax.optimization_barrier(jnp.mean(stream_f32 * stream_f32, axis=-1, keepdims=True)) + EPSILON)).astype(jnp.bfloat16)
    normed_blk = normed.reshape(N_EXP, N_BLK, TOK_DEV, D)
    stream_blk = stream.reshape(N_EXP, N_BLK, TOK_DEV, D)
    routes_blk = routes.reshape(N_EXP, N_BLK, TOK_DEV, TOPK)
    weight_blk = route_weight.reshape(N_EXP, N_BLK, TOK_DEV, TOPK)

    def per_blk(blk_idx):
        return experts_row(normed_blk[:, blk_idx], routes_blk[:, blk_idx], weight_blk[:, blk_idx], stream_blk[:, blk_idx], gate_up_weight, down_weight)
    layer = lax.map(per_blk, jnp.arange(N_BLK, dtype=jnp.int32))
    layer_out = jnp.transpose(layer, (1, 0, 2, 3)).reshape(N_EXP, SUFFIX, D)
    cache_pages = jax.vmap(regroup)(prompt_kv, page_owner)
    return (attended, layer_out, cache_pages)
```

```python
import jax
import jax.numpy as jnp
from jax import lax
from jax.sharding import PartitionSpec as P

D = 1024
H = 16
KVH = 8
HD = 64
FF = 512
TOPK = 8
EXP_DEV = 1
KB = 32
PAGE = 8


SCALE = 0.125
NEGATIVE = -1e30
EPSILON = 1e-06


def segment_of(lengths, count):
    ends = jnp.cumsum(lengths)
    position = jnp.arange(count, dtype=jnp.int32)
    return jnp.sum((position[:, None] >= ends[None, :]).astype(jnp.int32), axis=1)


def rank_within(labels, count):
    onehot = (labels[:, None] == jnp.arange(count, dtype=jnp.int32)[None, :]).astype(jnp.int32)
    before = jnp.cumsum(onehot, axis=0) - onehot
    return jnp.sum(before * onehot, axis=1)


def gather_rows(piece, axis):
    count = lax.axis_size(axis)
    tiles = jnp.broadcast_to(piece[None], (count,) + piece.shape)
    whole = lax.all_to_all(tiles, axis, split_axis=0, concat_axis=0, tiled=True)
    return whole.reshape((count * piece.shape[0],) + piece.shape[1:])


def absorb(carry_state, query_heads, key_heads, value_heads, visible):
    running_max, denom, numerator = carry_state
    scores = (
        jnp.einsum("tkgd,skd->tkgs", query_heads, key_heads, preferred_element_type=jnp.float32)
        * SCALE
    )
    new_max = jnp.maximum(running_max, jnp.max(jnp.where(visible, scores, NEGATIVE), axis=-1))
    factor = jnp.exp(running_max - new_max)
    weight = jnp.where(visible, jnp.exp(scores - new_max[..., None]), 0.0)
    denom = denom * factor + jnp.sum(weight, axis=-1)
    added = jnp.einsum(
        "tkgs,skd->tkgd",
        weight.astype(jnp.bfloat16),
        value_heads,
        preferred_element_type=jnp.float32,
    )
    numerator = numerator * factor[..., None] + added
    return (new_max, denom, numerator)


def local(
    residual,
    queries,
    suffix_kv,
    prompt_kv,
    prompt_lengths,
    block_keep,
    suffix_lengths,
    out_weight,
    routes,
    route_weight,
    gate_up_weight,
    down_weight,
    page_owner,
):
    tok_rows = queries.shape[1]
    kv_width = suffix_kv.shape[2] // 2
    group_size = H // KVH
    query_heads = queries[0].reshape(tok_rows, KVH, group_size, HD)
    own_keys = suffix_kv[0, :, :kv_width].reshape(tok_rows, KVH, HD)
    own_values = suffix_kv[0, :, kv_width:].reshape(tok_rows, KVH, HD)
    segment = segment_of(suffix_lengths[0, 0], tok_rows)
    position = jnp.arange(tok_rows, dtype=jnp.int32)
    own_seen = ((segment[:, None] == segment[None, :]) & (position[None, :] <= position[:, None]))[
        :, None, None, :
    ]
    start_state = (
        jnp.full((tok_rows, KVH, group_size), NEGATIVE, jnp.float32),
        jnp.zeros((tok_rows, KVH, group_size), jnp.float32),
        jnp.zeros((tok_rows, KVH, group_size, HD), jnp.float32),
    )
    carry_state = absorb(start_state, query_heads, own_keys, own_values, own_seen)
    block_rows = prompt_kv.shape[1]
    keep_rows = jnp.repeat(block_keep[0], KB)
    position_abs = lax.axis_index("blk") * block_rows + jnp.arange(block_rows, dtype=jnp.int32)
    live_keys = ((keep_rows > 0) & (position_abs < prompt_lengths[0])).astype(jnp.int32)[None, :]
    piece_kv = lax.all_gather(prompt_kv, "blk", axis=1, tiled=True)
    piece_live = lax.all_gather(live_keys, "blk", axis=1, tiled=True)
    count = piece_kv.shape[1]
    key_heads = piece_kv[0, :, :kv_width].reshape(count, KVH, HD)
    value_heads = piece_kv[0, :, kv_width:].reshape(count, KVH, HD)
    visible = (piece_live[0] > 0)[None, None, None, :]
    running_max, denom, numerator = absorb(
        carry_state, query_heads, key_heads, value_heads, visible
    )
    attended = (numerator / denom[..., None]).reshape(tok_rows, H * HD).astype(jnp.bfloat16)
    projected = jnp.dot(
        attended,
        gather_rows(out_weight, "exp"),
        preferred_element_type=jnp.float32,
    )
    stream = (residual[0].astype(jnp.float32) + projected).astype(jnp.bfloat16)
    stream_f32 = stream.astype(jnp.float32)
    normed = (
        stream_f32 * lax.rsqrt(jnp.mean(stream_f32 * stream_f32, axis=-1, keepdims=True) + EPSILON)
    ).astype(jnp.bfloat16)
    exp_count = lax.axis_size("exp")
    experts = EXP_DEV * exp_count
    capacity = min(tok_rows, 5 * tok_rows * TOPK // (4 * experts))
    flat_routes = routes[0].reshape(-1)
    slot_index = flat_routes * capacity + rank_within(flat_routes, experts)
    dispatch = (
        jnp.zeros((experts * capacity, D), jnp.bfloat16)
        .at[slot_index]
        .set(jnp.repeat(normed, TOPK, axis=0))
    )
    dispatch = dispatch.reshape(experts, capacity, D)
    arrived = lax.all_to_all(dispatch, "exp", split_axis=0, concat_axis=0, tiled=True)
    count = arrived.shape[1]
    grouped = arrived.reshape(exp_count, EXP_DEV, count, D)
    picked_rows = grouped[:, 0].reshape(exp_count * count, D)
    gate_up = jnp.dot(picked_rows, gate_up_weight[0], preferred_element_type=jnp.float32)
    hidden = (jax.nn.silu(gate_up[:, :FF]) * gate_up[:, FF:]).astype(jnp.bfloat16)
    result = jnp.dot(hidden, down_weight[0], preferred_element_type=jnp.float32).astype(
        jnp.bfloat16
    )
    results = [result.reshape(exp_count, count, D)]
    outgoing = jnp.stack(results, axis=1).reshape(exp_count * EXP_DEV, count, D)
    returned = lax.all_to_all(outgoing, "exp", split_axis=0, concat_axis=0, tiled=True)
    picked = (
        returned.reshape(experts * capacity, D)[slot_index]
        .astype(jnp.float32)
        .reshape(tok_rows, TOPK, D)
    )
    layer_out = (stream_f32 + jnp.sum(picked * route_weight[0][:, :, None], axis=1)).astype(
        jnp.bfloat16
    )
    page_count = block_rows // PAGE
    blk_count = lax.axis_size("blk")
    page_capacity = max(2, 2 * page_count // blk_count)
    page_rows = prompt_kv[0].reshape(page_count, PAGE, 2 * kv_width)
    owners = page_owner[0, :, 0]
    page_slot = owners * page_capacity + rank_within(owners, blk_count)
    outgoing_pages = (
        jnp.zeros((blk_count * page_capacity, PAGE, 2 * kv_width), jnp.bfloat16)
        .at[page_slot]
        .set(page_rows)
    )
    arrived_pages = lax.all_to_all(outgoing_pages, "blk", split_axis=0, concat_axis=0, tiled=True)
    cache_pages = arrived_pages.reshape(1, blk_count * page_capacity * PAGE, 2 * kv_width)
    return (attended[None], layer_out[None], cache_pages)


def solution(mesh):
    return jax.shard_map(
        local,
        mesh=mesh,
        in_specs=(
            P("exp", "blk", None),
            P("exp", "blk", None),
            P("exp", "blk", None),
            P("exp", "blk", None),
            P("exp"),
            P("exp", "blk"),
            P("exp", "blk", None),
            P("exp", None),
            P("exp", "blk", None),
            P("exp", "blk", None),
            P("exp", None, None),
            P("exp", None, None),
            P("exp", "blk", None),
        ),
        out_specs=(P("exp", "blk", None), P("exp", "blk", None), P("exp", "blk", None)),
        check_vma=False,
    )
```

```python
import jax
import jax.numpy as jnp
from jax import lax
from jax.sharding import PartitionSpec as P

D = 1024
H = 16
KVH = 8
HD = 64
FF = 512
TOPK = 8
EXP_DEV = 1
KB = 32
PAGE = 8


SCALE = 0.125
NEGATIVE = -1e30
EPSILON = 1e-06


def segment_of(lengths, count):
    ends = jnp.cumsum(lengths)
    position = jnp.arange(count, dtype=jnp.int32)
    return jnp.sum((position[:, None] >= ends[None, :]).astype(jnp.int32), axis=1)


def rank_within(labels, count):
    onehot = (labels[:, None] == jnp.arange(count, dtype=jnp.int32)[None, :]).astype(jnp.int32)
    before = jnp.cumsum(onehot, axis=0) - onehot
    return jnp.sum(before * onehot, axis=1)


def gather_rows(piece, axis):
    count = lax.axis_size(axis)
    tiles = jnp.broadcast_to(piece[None], (count,) + piece.shape)
    whole = lax.all_to_all(tiles, axis, split_axis=0, concat_axis=0, tiled=True)
    return whole.reshape((count * piece.shape[0],) + piece.shape[1:])


def absorb(carry_state, query_heads, key_heads, value_heads, visible):
    running_max, denom, numerator = carry_state
    scores = (
        jnp.einsum("tkgd,skd->tkgs", query_heads, key_heads, preferred_element_type=jnp.float32)
        * SCALE
    )
    new_max = jnp.maximum(running_max, jnp.max(jnp.where(visible, scores, NEGATIVE), axis=-1))
    factor = jnp.exp(running_max - new_max)
    weight = jnp.where(visible, jnp.exp(scores - new_max[..., None]), 0.0)
    denom = denom * factor + jnp.sum(weight, axis=-1)
    added = jnp.einsum(
        "tkgs,skd->tkgd",
        weight.astype(jnp.bfloat16),
        value_heads,
        preferred_element_type=jnp.float32,
    )
    numerator = numerator * factor[..., None] + added
    return (new_max, denom, numerator)


def local(
    residual,
    queries,
    suffix_kv,
    prompt_kv,
    prompt_lengths,
    block_keep,
    suffix_lengths,
    out_weight,
    routes,
    route_weight,
    gate_up_weight,
    down_weight,
    page_owner,
):
    tok_rows = queries.shape[1]
    kv_width = suffix_kv.shape[2] // 2
    group_size = H // KVH
    query_heads = queries[0].reshape(tok_rows, KVH, group_size, HD)
    own_keys = suffix_kv[0, :, :kv_width].reshape(tok_rows, KVH, HD)
    own_values = suffix_kv[0, :, kv_width:].reshape(tok_rows, KVH, HD)
    segment = segment_of(suffix_lengths[0, 0], tok_rows)
    position = jnp.arange(tok_rows, dtype=jnp.int32)
    own_seen = ((segment[:, None] == segment[None, :]) & (position[None, :] <= position[:, None]))[
        :, None, None, :
    ]
    start_state = (
        jnp.full((tok_rows, KVH, group_size), NEGATIVE, jnp.float32),
        jnp.zeros((tok_rows, KVH, group_size), jnp.float32),
        jnp.zeros((tok_rows, KVH, group_size, HD), jnp.float32),
    )
    carry_state = absorb(start_state, query_heads, own_keys, own_values, own_seen)
    block_rows = prompt_kv.shape[1]
    keep_rows = jnp.repeat(block_keep[0], KB)
    position_abs = lax.axis_index("blk") * block_rows + jnp.arange(block_rows, dtype=jnp.int32)
    live_keys = ((keep_rows > 0) & (position_abs < prompt_lengths[0])).astype(jnp.int32)[None, :]
    piece_kv = lax.all_gather(prompt_kv, "blk", axis=1, tiled=True)
    blk_count = lax.axis_size("blk")
    page_count = block_rows // PAGE
    packed = jnp.concatenate([live_keys[0], page_owner[0, :, 0]])
    packed_all = lax.all_gather(packed, "blk", axis=0, tiled=True).reshape(blk_count, -1)
    piece_live = packed_all[:, :block_rows].reshape(1, -1)
    owners_all = packed_all[:, block_rows:]
    count = piece_kv.shape[1]
    key_heads = piece_kv[0, :, :kv_width].reshape(count, KVH, HD)
    value_heads = piece_kv[0, :, kv_width:].reshape(count, KVH, HD)
    visible = (piece_live[0] > 0)[None, None, None, :]
    running_max, denom, numerator = absorb(
        carry_state, query_heads, key_heads, value_heads, visible
    )
    attended = (numerator / denom[..., None]).reshape(tok_rows, H * HD).astype(jnp.bfloat16)
    projected = jnp.dot(
        attended,
        gather_rows(out_weight, "exp"),
        preferred_element_type=jnp.float32,
    )
    stream = (residual[0].astype(jnp.float32) + projected).astype(jnp.bfloat16)
    stream_f32 = stream.astype(jnp.float32)
    normed = (
        stream_f32 * lax.rsqrt(jnp.mean(stream_f32 * stream_f32, axis=-1, keepdims=True) + EPSILON)
    ).astype(jnp.bfloat16)
    exp_count = lax.axis_size("exp")
    experts = EXP_DEV * exp_count
    capacity = min(tok_rows, 5 * tok_rows * TOPK // (4 * experts))
    flat_routes = routes[0].reshape(-1)
    slot_index = flat_routes * capacity + rank_within(flat_routes, experts)
    slot_iota = jnp.arange(experts * capacity, dtype=jnp.int32)
    token_slots = slot_index.reshape(tok_rows, TOPK)
    hits = token_slots[None, :, :] == slot_iota[:, None, None]
    placer = jnp.any(hits, axis=-1).astype(jnp.bfloat16)
    dispatch = jnp.dot(placer, normed, preferred_element_type=jnp.float32).astype(jnp.bfloat16)
    dispatch = dispatch.reshape(experts, capacity, D)
    arrived = lax.all_to_all(dispatch, "exp", split_axis=0, concat_axis=0, tiled=True)
    count = arrived.shape[1]
    grouped = arrived.reshape(exp_count, EXP_DEV, count, D)
    picked_rows = grouped[:, 0].reshape(exp_count * count, D)
    gate_up = jnp.dot(picked_rows, gate_up_weight[0], preferred_element_type=jnp.float32)
    hidden = (jax.nn.silu(gate_up[:, :FF]) * gate_up[:, FF:]).astype(jnp.bfloat16)
    result = jnp.dot(hidden, down_weight[0], preferred_element_type=jnp.float32).astype(
        jnp.bfloat16
    )
    results = [result.reshape(exp_count, count, D)]
    outgoing = jnp.stack(results, axis=1).reshape(exp_count * EXP_DEV, count, D)
    returned = lax.all_to_all(outgoing, "exp", split_axis=0, concat_axis=0, tiled=True)
    slot_weight = jnp.sum(
        jnp.where(
            token_slots[:, :, None] == slot_iota[None, None, :],
            route_weight[0][:, :, None],
            0.0,
        ),
        axis=1,
    )
    combined = jnp.dot(
        slot_weight,
        returned.reshape(experts * capacity, D).astype(jnp.float32),
        precision=lax.Precision.HIGHEST,
        preferred_element_type=jnp.float32,
    )
    layer_out = (stream_f32 + combined).astype(jnp.bfloat16)
    page_capacity = max(2, 2 * page_count // blk_count)
    me = lax.axis_index("blk")
    page_rank = jax.vmap(lambda labels: rank_within(labels, blk_count))(owners_all)
    block_of = jnp.arange(blk_count, dtype=jnp.int32)[:, None]
    page_slot = jnp.where(owners_all == me, block_of * page_capacity + page_rank, -1).reshape(-1)
    out_rows = blk_count * page_capacity * PAGE
    row_slot = jnp.arange(out_rows, dtype=jnp.int32) // PAGE
    prompt_rows = piece_kv.shape[1]
    src_page = jnp.arange(prompt_rows, dtype=jnp.int32) // PAGE
    same_row = (jnp.arange(out_rows)[:, None] % PAGE) == (jnp.arange(prompt_rows)[None, :] % PAGE)
    chooser = (page_slot[src_page][None, :] == row_slot[:, None]) & same_row
    cache_pages = jnp.dot(
        chooser.astype(jnp.bfloat16), piece_kv[0], preferred_element_type=jnp.float32
    ).astype(jnp.bfloat16)[None]
    return (attended[None], layer_out[None], cache_pages)


def solution(mesh):
    return jax.shard_map(
        local,
        mesh=mesh,
        in_specs=(
            P("exp", "blk", None),
            P("exp", "blk", None),
            P("exp", "blk", None),
            P("exp", "blk", None),
            P("exp"),
            P("exp", "blk"),
            P("exp", "blk", None),
            P("exp", None),
            P("exp", "blk", None),
            P("exp", "blk", None),
            P("exp", None, None),
            P("exp", None, None),
            P("exp", "blk", None),
        ),
        out_specs=(P("exp", "blk", None), P("exp", "blk", None), P("exp", "blk", None)),
        check_vma=False,
    )
```

```python
import jax
import jax.numpy as jnp
from jax import lax
from jax.sharding import PartitionSpec as P

D = 1024
H = 16
KVH = 8
HD = 64
FF = 512
TOPK = 8
EXP_DEV = 1
KB = 32
PAGE = 8


SCALE = 0.125
NEGATIVE = -1e30
EPSILON = 1e-06


def segment_of(lengths, count):
    ends = jnp.cumsum(lengths)
    position = jnp.arange(count, dtype=jnp.int32)
    return jnp.sum((position[:, None] >= ends[None, :]).astype(jnp.int32), axis=1)


def rank_within(labels, count):
    onehot = (labels[:, None] == jnp.arange(count, dtype=jnp.int32)[None, :]).astype(jnp.int32)
    before = jnp.cumsum(onehot, axis=0) - onehot
    return jnp.sum(before * onehot, axis=1)


def gather_rows(piece, axis):
    count = lax.axis_size(axis)
    tiles = jnp.broadcast_to(piece[None], (count,) + piece.shape)
    whole = lax.all_to_all(tiles, axis, split_axis=0, concat_axis=0, tiled=True)
    return whole.reshape((count * piece.shape[0],) + piece.shape[1:])


def gather_shifts(piece, axis):
    count = lax.axis_size(axis)
    parts = [piece]
    for shift in range(1, count):
        pairs = [(j, (j + shift) % count) for j in range(count)]
        parts.append(lax.ppermute(piece, axis, pairs))
    return jnp.stack(parts)


def absorb(carry_state, query_heads, key_heads, value_heads, visible):
    running_max, denom, numerator = carry_state
    scores = (
        jnp.einsum("tkgd,skd->tkgs", query_heads, key_heads, preferred_element_type=jnp.float32)
        * SCALE
    )
    new_max = jnp.maximum(running_max, jnp.max(jnp.where(visible, scores, NEGATIVE), axis=-1))
    factor = jnp.exp(running_max - new_max)
    weight = jnp.where(visible, jnp.exp(scores - new_max[..., None]), 0.0)
    denom = denom * factor + jnp.sum(weight, axis=-1)
    added = jnp.einsum(
        "tkgs,skd->tkgd",
        weight.astype(jnp.bfloat16),
        value_heads,
        preferred_element_type=jnp.float32,
    )
    numerator = numerator * factor[..., None] + added
    return (new_max, denom, numerator)


def local(
    residual,
    queries,
    suffix_kv,
    prompt_kv,
    prompt_lengths,
    block_keep,
    suffix_lengths,
    out_weight,
    routes,
    route_weight,
    gate_up_weight,
    down_weight,
    page_owner,
):
    tok_rows = queries.shape[1]
    kv_width = suffix_kv.shape[2] // 2
    group_size = H // KVH
    query_heads = queries[0].reshape(tok_rows, KVH, group_size, HD)
    own_keys = suffix_kv[0, :, :kv_width].reshape(tok_rows, KVH, HD)
    own_values = suffix_kv[0, :, kv_width:].reshape(tok_rows, KVH, HD)
    segment = segment_of(suffix_lengths[0, 0], tok_rows)
    position = jnp.arange(tok_rows, dtype=jnp.int32)
    own_seen = ((segment[:, None] == segment[None, :]) & (position[None, :] <= position[:, None]))[
        :, None, None, :
    ]
    start_state = (
        jnp.full((tok_rows, KVH, group_size), NEGATIVE, jnp.float32),
        jnp.zeros((tok_rows, KVH, group_size), jnp.float32),
        jnp.zeros((tok_rows, KVH, group_size, HD), jnp.float32),
    )
    carry_state = absorb(start_state, query_heads, own_keys, own_values, own_seen)
    block_rows = prompt_kv.shape[1]
    keep_rows = jnp.repeat(block_keep[0], KB)
    position_abs = lax.axis_index("blk") * block_rows + jnp.arange(block_rows, dtype=jnp.int32)
    live_keys = ((keep_rows > 0) & (position_abs < prompt_lengths[0])).astype(jnp.int32)[None, :]
    blk_count = lax.axis_size("blk")
    me = lax.axis_index("blk")
    piece_kv = gather_shifts(prompt_kv[0], "blk").reshape(1, blk_count * block_rows, -1)
    source_of = (me - jnp.arange(blk_count, dtype=jnp.int32)) % blk_count
    global_row = (source_of[:, None] * block_rows + jnp.arange(block_rows, dtype=jnp.int32)).reshape(-1)
    page_count = block_rows // PAGE
    packed = jnp.concatenate([live_keys[0], page_owner[0, :, 0]])
    packed_all = lax.all_gather(packed, "blk", axis=0, tiled=True).reshape(blk_count, -1)
    piece_live = packed_all[:, :block_rows].reshape(-1)[global_row][None]
    owners_all = packed_all[:, block_rows:]
    count = piece_kv.shape[1]
    key_heads = piece_kv[0, :, :kv_width].reshape(count, KVH, HD)
    value_heads = piece_kv[0, :, kv_width:].reshape(count, KVH, HD)
    visible = (piece_live[0] > 0)[None, None, None, :]
    running_max, denom, numerator = absorb(
        carry_state, query_heads, key_heads, value_heads, visible
    )
    attended = (numerator / denom[..., None]).reshape(tok_rows, H * HD).astype(jnp.bfloat16)
    projected = jnp.dot(
        attended,
        gather_rows(out_weight, "exp"),
        preferred_element_type=jnp.float32,
    )
    stream = (residual[0].astype(jnp.float32) + projected).astype(jnp.bfloat16)
    stream_f32 = stream.astype(jnp.float32)
    normed = (
        stream_f32 * lax.rsqrt(jnp.mean(stream_f32 * stream_f32, axis=-1, keepdims=True) + EPSILON)
    ).astype(jnp.bfloat16)
    exp_count = lax.axis_size("exp")
    experts = EXP_DEV * exp_count
    capacity = min(tok_rows, 5 * tok_rows * TOPK // (4 * experts))
    flat_routes = routes[0].reshape(-1)
    slot_index = flat_routes * capacity + rank_within(flat_routes, experts)
    slot_iota = jnp.arange(experts * capacity, dtype=jnp.int32)
    token_slots = slot_index.reshape(tok_rows, TOPK)
    hits = token_slots[None, :, :] == slot_iota[:, None, None]
    placer = jnp.any(hits, axis=-1).astype(jnp.bfloat16)
    dispatch = jnp.dot(placer, normed, preferred_element_type=jnp.float32).astype(jnp.bfloat16)
    dispatch = dispatch.reshape(experts, capacity, D)
    arrived = lax.all_to_all(dispatch, "exp", split_axis=0, concat_axis=0, tiled=True)
    count = arrived.shape[1]
    grouped = arrived.reshape(exp_count, EXP_DEV, count, D)
    picked_rows = grouped[:, 0].reshape(exp_count * count, D)
    gate_up = jnp.dot(picked_rows, gate_up_weight[0], preferred_element_type=jnp.float32)
    hidden = (jax.nn.silu(gate_up[:, :FF]) * gate_up[:, FF:]).astype(jnp.bfloat16)
    result = jnp.dot(hidden, down_weight[0], preferred_element_type=jnp.float32).astype(
        jnp.bfloat16
    )
    results = [result.reshape(exp_count, count, D)]
    outgoing = jnp.stack(results, axis=1).reshape(exp_count * EXP_DEV, count, D)
    returned = lax.all_to_all(outgoing, "exp", split_axis=0, concat_axis=0, tiled=True)
    slot_weight = jnp.sum(
        jnp.where(
            token_slots[:, :, None] == slot_iota[None, None, :],
            route_weight[0][:, :, None],
            0.0,
        ),
        axis=1,
    )
    combined = jnp.dot(
        slot_weight,
        returned.reshape(experts * capacity, D).astype(jnp.float32),
        precision=lax.Precision.HIGHEST,
        preferred_element_type=jnp.float32,
    )
    layer_out = (stream_f32 + combined).astype(jnp.bfloat16)
    page_capacity = max(2, 2 * page_count // blk_count)
    page_rank = jax.vmap(lambda labels: rank_within(labels, blk_count))(owners_all)
    block_of = jnp.arange(blk_count, dtype=jnp.int32)[:, None]
    page_slot = jnp.where(owners_all == me, block_of * page_capacity + page_rank, -1).reshape(-1)
    out_rows = blk_count * page_capacity * PAGE
    row_slot = jnp.arange(out_rows, dtype=jnp.int32) // PAGE
    prompt_rows = piece_kv.shape[1]
    src_page = global_row // PAGE
    same_row = (jnp.arange(out_rows)[:, None] % PAGE) == (jnp.arange(prompt_rows)[None, :] % PAGE)
    chooser = (page_slot[src_page][None, :] == row_slot[:, None]) & same_row
    cache_pages = jnp.dot(
        chooser.astype(jnp.bfloat16), piece_kv[0], preferred_element_type=jnp.float32
    ).astype(jnp.bfloat16)[None]
    return (attended[None], layer_out[None], cache_pages)


def solution(mesh):
    return jax.shard_map(
        local,
        mesh=mesh,
        in_specs=(
            P("exp", "blk", None),
            P("exp", "blk", None),
            P("exp", "blk", None),
            P("exp", "blk", None),
            P("exp"),
            P("exp", "blk"),
            P("exp", "blk", None),
            P("exp", None),
            P("exp", "blk", None),
            P("exp", "blk", None),
            P("exp", None, None),
            P("exp", None, None),
            P("exp", "blk", None),
        ),
        out_specs=(P("exp", "blk", None), P("exp", "blk", None), P("exp", "blk", None)),
        check_vma=False,
    )
```

```python
import jax
import jax.numpy as jnp
from jax import lax
from jax.sharding import PartitionSpec as P

D = 1024
H = 16
KVH = 8
HD = 64
FF = 512
TOPK = 8
EXP_DEV = 1
KB = 32
PAGE = 8


SCALE = 0.125
NEGATIVE = -1e30
EPSILON = 1e-06


def segment_of(lengths, count):
    ends = jnp.cumsum(lengths)
    position = jnp.arange(count, dtype=jnp.int32)
    return jnp.sum((position[:, None] >= ends[None, :]).astype(jnp.int32), axis=1)


def rank_within(labels, count):
    onehot = (labels[:, None] == jnp.arange(count, dtype=jnp.int32)[None, :]).astype(jnp.int32)
    before = jnp.cumsum(onehot, axis=0) - onehot
    return jnp.sum(before * onehot, axis=1)


def gather_rows(piece, axis):
    count = lax.axis_size(axis)
    tiles = jnp.broadcast_to(piece[None], (count,) + piece.shape)
    whole = lax.all_to_all(tiles, axis, split_axis=0, concat_axis=0, tiled=True)
    return whole.reshape((count * piece.shape[0],) + piece.shape[1:])


def absorb(carry_state, query_heads, key_heads, value_heads, visible):
    running_max, denom, numerator = carry_state
    scores = (
        jnp.einsum("tkgd,skd->tkgs", query_heads, key_heads, preferred_element_type=jnp.float32)
        * SCALE
    )
    new_max = jnp.maximum(running_max, jnp.max(jnp.where(visible, scores, NEGATIVE), axis=-1))
    factor = jnp.exp(running_max - new_max)
    weight = jnp.where(visible, jnp.exp(scores - new_max[..., None]), 0.0)
    denom = denom * factor + jnp.sum(weight, axis=-1)
    added = jnp.einsum(
        "tkgs,skd->tkgd",
        weight.astype(jnp.bfloat16),
        value_heads,
        preferred_element_type=jnp.float32,
    )
    numerator = numerator * factor[..., None] + added
    return (new_max, denom, numerator)


def local(
    residual,
    queries,
    suffix_kv,
    prompt_kv,
    prompt_lengths,
    block_keep,
    suffix_lengths,
    out_weight,
    routes,
    route_weight,
    gate_up_weight,
    down_weight,
    page_owner,
):
    tok_rows = queries.shape[1]
    kv_width = suffix_kv.shape[2] // 2
    group_size = H // KVH
    query_heads = queries[0].reshape(tok_rows, KVH, group_size, HD)
    own_keys = suffix_kv[0, :, :kv_width].reshape(tok_rows, KVH, HD)
    own_values = suffix_kv[0, :, kv_width:].reshape(tok_rows, KVH, HD)
    segment = segment_of(suffix_lengths[0, 0], tok_rows)
    position = jnp.arange(tok_rows, dtype=jnp.int32)
    own_seen = ((segment[:, None] == segment[None, :]) & (position[None, :] <= position[:, None]))[
        :, None, None, :
    ]
    start_state = (
        jnp.full((tok_rows, KVH, group_size), NEGATIVE, jnp.float32),
        jnp.zeros((tok_rows, KVH, group_size), jnp.float32),
        jnp.zeros((tok_rows, KVH, group_size, HD), jnp.float32),
    )
    carry_state = absorb(start_state, query_heads, own_keys, own_values, own_seen)
    block_rows = prompt_kv.shape[1]
    keep_rows = jnp.repeat(block_keep[0], KB)
    position_abs = lax.axis_index("blk") * block_rows + jnp.arange(block_rows, dtype=jnp.int32)
    live_keys = ((keep_rows > 0) & (position_abs < prompt_lengths[0])).astype(jnp.int32)[None, :]
    piece_kv = gather_rows(prompt_kv[0], "blk")[None]
    blk_count = lax.axis_size("blk")
    page_count = block_rows // PAGE
    packed = jnp.concatenate([live_keys[0], page_owner[0, :, 0]])
    packed_all = lax.all_gather(packed, "blk", axis=0, tiled=True).reshape(blk_count, -1)
    piece_live = packed_all[:, :block_rows].reshape(1, -1)
    owners_all = packed_all[:, block_rows:]
    count = piece_kv.shape[1]
    key_heads = piece_kv[0, :, :kv_width].reshape(count, KVH, HD)
    value_heads = piece_kv[0, :, kv_width:].reshape(count, KVH, HD)
    visible = (piece_live[0] > 0)[None, None, None, :]
    running_max, denom, numerator = absorb(
        carry_state, query_heads, key_heads, value_heads, visible
    )
    attended = (numerator / denom[..., None]).reshape(tok_rows, H * HD).astype(jnp.bfloat16)
    projected = jnp.dot(
        attended,
        lax.all_gather(out_weight, "exp", axis=0, tiled=True),
        preferred_element_type=jnp.float32,
    )
    stream = (residual[0].astype(jnp.float32) + projected).astype(jnp.bfloat16)
    stream_f32 = stream.astype(jnp.float32)
    normed = (
        stream_f32 * lax.rsqrt(jnp.mean(stream_f32 * stream_f32, axis=-1, keepdims=True) + EPSILON)
    ).astype(jnp.bfloat16)
    exp_count = lax.axis_size("exp")
    experts = EXP_DEV * exp_count
    capacity = min(tok_rows, 5 * tok_rows * TOPK // (4 * experts))
    flat_routes = routes[0].reshape(-1)
    slot_index = flat_routes * capacity + rank_within(flat_routes, experts)
    slot_iota = jnp.arange(experts * capacity, dtype=jnp.int32)
    token_slots = slot_index.reshape(tok_rows, TOPK)
    hits = token_slots[None, :, :] == slot_iota[:, None, None]
    placer = jnp.any(hits, axis=-1).astype(jnp.bfloat16)
    dispatch = jnp.dot(placer, normed, preferred_element_type=jnp.float32).astype(jnp.bfloat16)
    dispatch = dispatch.reshape(experts, capacity, D)
    arrived = lax.all_to_all(dispatch, "exp", split_axis=0, concat_axis=0, tiled=True)
    count = arrived.shape[1]
    grouped = arrived.reshape(exp_count, EXP_DEV, count, D)
    picked_rows = grouped[:, 0].reshape(exp_count * count, D)
    gate_up = jnp.dot(picked_rows, gate_up_weight[0], preferred_element_type=jnp.float32)
    hidden = (jax.nn.silu(gate_up[:, :FF]) * gate_up[:, FF:]).astype(jnp.bfloat16)
    result = jnp.dot(hidden, down_weight[0], preferred_element_type=jnp.float32).astype(
        jnp.bfloat16
    )
    results = [result.reshape(exp_count, count, D)]
    outgoing = jnp.stack(results, axis=1).reshape(exp_count * EXP_DEV, count, D)
    returned = lax.all_to_all(outgoing, "exp", split_axis=0, concat_axis=0, tiled=True)
    slot_weight = jnp.sum(
        jnp.where(
            token_slots[:, :, None] == slot_iota[None, None, :],
            route_weight[0][:, :, None],
            0.0,
        ),
        axis=1,
    )
    combined = jnp.dot(
        slot_weight,
        returned.reshape(experts * capacity, D).astype(jnp.float32),
        precision=lax.Precision.HIGHEST,
        preferred_element_type=jnp.float32,
    )
    layer_out = (stream_f32 + combined).astype(jnp.bfloat16)
    page_capacity = max(2, 2 * page_count // blk_count)
    me = lax.axis_index("blk")
    page_rank = jax.vmap(lambda labels: rank_within(labels, blk_count))(owners_all)
    block_of = jnp.arange(blk_count, dtype=jnp.int32)[:, None]
    page_slot = jnp.where(owners_all == me, block_of * page_capacity + page_rank, -1).reshape(-1)
    out_rows = blk_count * page_capacity * PAGE
    row_slot = jnp.arange(out_rows, dtype=jnp.int32) // PAGE
    prompt_rows = piece_kv.shape[1]
    src_page = jnp.arange(prompt_rows, dtype=jnp.int32) // PAGE
    same_row = (jnp.arange(out_rows)[:, None] % PAGE) == (jnp.arange(prompt_rows)[None, :] % PAGE)
    chooser = (page_slot[src_page][None, :] == row_slot[:, None]) & same_row
    cache_pages = jnp.dot(
        chooser.astype(jnp.bfloat16), piece_kv[0], preferred_element_type=jnp.float32
    ).astype(jnp.bfloat16)[None]
    return (attended[None], layer_out[None], cache_pages)


def solution(mesh):
    return jax.shard_map(
        local,
        mesh=mesh,
        in_specs=(
            P("exp", "blk", None),
            P("exp", "blk", None),
            P("exp", "blk", None),
            P("exp", "blk", None),
            P("exp"),
            P("exp", "blk"),
            P("exp", "blk", None),
            P("exp", None),
            P("exp", "blk", None),
            P("exp", "blk", None),
            P("exp", None, None),
            P("exp", None, None),
            P("exp", "blk", None),
        ),
        out_specs=(P("exp", "blk", None), P("exp", "blk", None), P("exp", "blk", None)),
        check_vma=False,
    )
```

```python
import jax
import jax.numpy as jnp
from jax import lax
from jax.sharding import PartitionSpec as P

D = 1024
H = 16
KVH = 8
HD = 64
FF = 512
TOPK = 8
EXP_DEV = 1
KB = 32
PAGE = 8


SCALE = 0.125
NEGATIVE = -1e30
EPSILON = 1e-06


def segment_of(lengths, count):
    ends = jnp.cumsum(lengths)
    position = jnp.arange(count, dtype=jnp.int32)
    return jnp.sum((position[:, None] >= ends[None, :]).astype(jnp.int32), axis=1)


def rank_within(labels, count):
    onehot = (labels[:, None] == jnp.arange(count, dtype=jnp.int32)[None, :]).astype(jnp.int32)
    before = jnp.cumsum(onehot, axis=0) - onehot
    return jnp.sum(before * onehot, axis=1)


def gather_rows(piece, axis):
    count = lax.axis_size(axis)
    tiles = jnp.broadcast_to(piece[None], (count,) + piece.shape)
    whole = lax.all_to_all(tiles, axis, split_axis=0, concat_axis=0, tiled=True)
    return whole.reshape((count * piece.shape[0],) + piece.shape[1:])


def absorb(carry_state, query_heads, key_heads, value_heads, visible):
    running_max, denom, numerator = carry_state
    scores = (
        jnp.einsum("tkgd,skd->tkgs", query_heads, key_heads, preferred_element_type=jnp.float32)
        * SCALE
    )
    new_max = jnp.maximum(running_max, jnp.max(jnp.where(visible, scores, NEGATIVE), axis=-1))
    factor = jnp.exp(running_max - new_max)
    weight = jnp.where(visible, jnp.exp(scores - new_max[..., None]), 0.0)
    denom = denom * factor + jnp.sum(weight, axis=-1)
    added = jnp.einsum(
        "tkgs,skd->tkgd",
        weight.astype(jnp.bfloat16),
        value_heads,
        preferred_element_type=jnp.float32,
    )
    numerator = numerator * factor[..., None] + added
    return (new_max, denom, numerator)


def local(
    residual,
    queries,
    suffix_kv,
    prompt_kv,
    prompt_lengths,
    block_keep,
    suffix_lengths,
    out_weight,
    routes,
    route_weight,
    gate_up_weight,
    down_weight,
    page_owner,
):
    tok_rows = queries.shape[1]
    kv_width = suffix_kv.shape[2] // 2
    group_size = H // KVH
    query_heads = queries[0].reshape(tok_rows, KVH, group_size, HD)
    own_keys = suffix_kv[0, :, :kv_width].reshape(tok_rows, KVH, HD)
    own_values = suffix_kv[0, :, kv_width:].reshape(tok_rows, KVH, HD)
    segment = segment_of(suffix_lengths[0, 0], tok_rows)
    position = jnp.arange(tok_rows, dtype=jnp.int32)
    own_seen = ((segment[:, None] == segment[None, :]) & (position[None, :] <= position[:, None]))[
        :, None, None, :
    ]
    start_state = (
        jnp.full((tok_rows, KVH, group_size), NEGATIVE, jnp.float32),
        jnp.zeros((tok_rows, KVH, group_size), jnp.float32),
        jnp.zeros((tok_rows, KVH, group_size, HD), jnp.float32),
    )
    carry_state = absorb(start_state, query_heads, own_keys, own_values, own_seen)
    block_rows = prompt_kv.shape[1]
    keep_rows = jnp.repeat(block_keep[0], KB)
    position_abs = lax.axis_index("blk") * block_rows + jnp.arange(block_rows, dtype=jnp.int32)
    live_keys = ((keep_rows > 0) & (position_abs < prompt_lengths[0])).astype(jnp.int32)[None, :]
    keys_all = lax.all_gather(prompt_kv[0, :, :kv_width], "blk", axis=0, tiled=True)
    values_local, keys_all = lax.optimization_barrier((prompt_kv[0, :, kv_width:], keys_all))
    values_all = lax.all_gather(values_local, "blk", axis=0, tiled=True)
    blk_count = lax.axis_size("blk")
    page_count = block_rows // PAGE
    packed = jnp.concatenate([live_keys[0], page_owner[0, :, 0]])
    packed_all = lax.all_gather(packed, "blk", axis=0, tiled=True).reshape(blk_count, -1)
    piece_live = packed_all[:, :block_rows].reshape(1, -1)
    owners_all = packed_all[:, block_rows:]
    count = keys_all.shape[0]
    key_heads = keys_all.reshape(count, KVH, HD)
    value_heads = values_all.reshape(count, KVH, HD)
    visible = (piece_live[0] > 0)[None, None, None, :]
    running_max, denom, numerator = absorb(
        carry_state, query_heads, key_heads, value_heads, visible
    )
    attended = (numerator / denom[..., None]).reshape(tok_rows, H * HD).astype(jnp.bfloat16)
    projected = jnp.dot(
        attended,
        gather_rows(out_weight, "exp"),
        preferred_element_type=jnp.float32,
    )
    stream = (residual[0].astype(jnp.float32) + projected).astype(jnp.bfloat16)
    stream_f32 = stream.astype(jnp.float32)
    normed = (
        stream_f32 * lax.rsqrt(jnp.mean(stream_f32 * stream_f32, axis=-1, keepdims=True) + EPSILON)
    ).astype(jnp.bfloat16)
    exp_count = lax.axis_size("exp")
    experts = EXP_DEV * exp_count
    capacity = min(tok_rows, 5 * tok_rows * TOPK // (4 * experts))
    flat_routes = routes[0].reshape(-1)
    slot_index = flat_routes * capacity + rank_within(flat_routes, experts)
    slot_iota = jnp.arange(experts * capacity, dtype=jnp.int32)
    token_slots = slot_index.reshape(tok_rows, TOPK)
    hits = token_slots[None, :, :] == slot_iota[:, None, None]
    placer = jnp.any(hits, axis=-1).astype(jnp.bfloat16)
    dispatch = jnp.dot(placer, normed, preferred_element_type=jnp.float32).astype(jnp.bfloat16)
    dispatch = dispatch.reshape(experts, capacity, D)
    arrived = lax.all_to_all(dispatch, "exp", split_axis=0, concat_axis=0, tiled=True)
    count = arrived.shape[1]
    grouped = arrived.reshape(exp_count, EXP_DEV, count, D)
    picked_rows = grouped[:, 0].reshape(exp_count * count, D)
    gate_up = jnp.dot(picked_rows, gate_up_weight[0], preferred_element_type=jnp.float32)
    hidden = (jax.nn.silu(gate_up[:, :FF]) * gate_up[:, FF:]).astype(jnp.bfloat16)
    result = jnp.dot(hidden, down_weight[0], preferred_element_type=jnp.float32).astype(
        jnp.bfloat16
    )
    results = [result.reshape(exp_count, count, D)]
    outgoing = jnp.stack(results, axis=1).reshape(exp_count * EXP_DEV, count, D)
    returned = lax.all_to_all(outgoing, "exp", split_axis=0, concat_axis=0, tiled=True)
    slot_weight = jnp.sum(
        jnp.where(
            token_slots[:, :, None] == slot_iota[None, None, :],
            route_weight[0][:, :, None],
            0.0,
        ),
        axis=1,
    )
    combined = jnp.dot(
        slot_weight,
        returned.reshape(experts * capacity, D).astype(jnp.float32),
        precision=lax.Precision.HIGHEST,
        preferred_element_type=jnp.float32,
    )
    layer_out = (stream_f32 + combined).astype(jnp.bfloat16)
    page_capacity = max(2, 2 * page_count // blk_count)
    me = lax.axis_index("blk")
    page_rank = jax.vmap(lambda labels: rank_within(labels, blk_count))(owners_all)
    block_of = jnp.arange(blk_count, dtype=jnp.int32)[:, None]
    page_slot = jnp.where(owners_all == me, block_of * page_capacity + page_rank, -1).reshape(-1)
    out_rows = blk_count * page_capacity * PAGE
    row_slot = jnp.arange(out_rows, dtype=jnp.int32) // PAGE
    prompt_rows = keys_all.shape[0]
    src_page = jnp.arange(prompt_rows, dtype=jnp.int32) // PAGE
    same_row = (jnp.arange(out_rows)[:, None] % PAGE) == (jnp.arange(prompt_rows)[None, :] % PAGE)
    chooser = (page_slot[src_page][None, :] == row_slot[:, None]) & same_row
    chooser = chooser.astype(jnp.bfloat16)
    cache_keys = jnp.dot(chooser, keys_all, preferred_element_type=jnp.float32)
    cache_values = jnp.dot(chooser, values_all, preferred_element_type=jnp.float32)
    cache_pages = jnp.concatenate([cache_keys, cache_values], axis=1).astype(jnp.bfloat16)[None]
    return (attended[None], layer_out[None], cache_pages)


def solution(mesh):
    return jax.shard_map(
        local,
        mesh=mesh,
        in_specs=(
            P("exp", "blk", None),
            P("exp", "blk", None),
            P("exp", "blk", None),
            P("exp", "blk", None),
            P("exp"),
            P("exp", "blk"),
            P("exp", "blk", None),
            P("exp", None),
            P("exp", "blk", None),
            P("exp", "blk", None),
            P("exp", None, None),
            P("exp", None, None),
            P("exp", "blk", None),
        ),
        out_specs=(P("exp", "blk", None), P("exp", "blk", None), P("exp", "blk", None)),
        check_vma=False,
    )
```

```python
import jax
import jax.numpy as jnp
from jax import lax
from jax.sharding import PartitionSpec as P

D = 1024
H = 16
KVH = 8
HD = 64
FF = 512
TOPK = 8
EXP_DEV = 1
KB = 32
PAGE = 8


SCALE = 0.125
NEGATIVE = -1e30
EPSILON = 1e-06


def segment_of(lengths, count):
    ends = jnp.cumsum(lengths)
    position = jnp.arange(count, dtype=jnp.int32)
    return jnp.sum((position[:, None] >= ends[None, :]).astype(jnp.int32), axis=1)


def rank_within(labels, count):
    onehot = (labels[:, None] == jnp.arange(count, dtype=jnp.int32)[None, :]).astype(jnp.int32)
    before = jnp.cumsum(onehot, axis=0) - onehot
    return jnp.sum(before * onehot, axis=1)


def gather_rows(piece, axis):
    count = lax.axis_size(axis)
    tiles = jnp.broadcast_to(piece[None], (count,) + piece.shape)
    whole = lax.all_to_all(tiles, axis, split_axis=0, concat_axis=0, tiled=True)
    return whole.reshape((count * piece.shape[0],) + piece.shape[1:])


def absorb(carry_state, query_heads, key_heads, value_heads, visible):
    running_max, denom, numerator = carry_state
    scores = (
        jnp.einsum("tkgd,skd->tkgs", query_heads, key_heads, preferred_element_type=jnp.float32)
        * SCALE
    )
    new_max = jnp.maximum(running_max, jnp.max(jnp.where(visible, scores, NEGATIVE), axis=-1))
    factor = jnp.exp(running_max - new_max)
    weight = jnp.where(visible, jnp.exp(scores - new_max[..., None]), 0.0)
    denom = denom * factor + jnp.sum(weight, axis=-1)
    added = jnp.einsum(
        "tkgs,skd->tkgd",
        weight.astype(jnp.bfloat16),
        value_heads,
        preferred_element_type=jnp.float32,
    )
    numerator = numerator * factor[..., None] + added
    return (new_max, denom, numerator)


def local(
    residual,
    queries,
    suffix_kv,
    prompt_kv,
    prompt_lengths,
    block_keep,
    suffix_lengths,
    out_weight,
    routes,
    route_weight,
    gate_up_weight,
    down_weight,
    page_owner,
):
    tok_rows = queries.shape[1]
    kv_width = suffix_kv.shape[2] // 2
    group_size = H // KVH
    query_heads = queries[0].reshape(tok_rows, KVH, group_size, HD)
    own_keys = suffix_kv[0, :, :kv_width].reshape(tok_rows, KVH, HD)
    own_values = suffix_kv[0, :, kv_width:].reshape(tok_rows, KVH, HD)
    segment = segment_of(suffix_lengths[0, 0], tok_rows)
    position = jnp.arange(tok_rows, dtype=jnp.int32)
    own_seen = ((segment[:, None] == segment[None, :]) & (position[None, :] <= position[:, None]))[
        :, None, None, :
    ]
    start_state = (
        jnp.full((tok_rows, KVH, group_size), NEGATIVE, jnp.float32),
        jnp.zeros((tok_rows, KVH, group_size), jnp.float32),
        jnp.zeros((tok_rows, KVH, group_size, HD), jnp.float32),
    )
    carry_state = absorb(start_state, query_heads, own_keys, own_values, own_seen)
    block_rows = prompt_kv.shape[1]
    keep_rows = jnp.repeat(block_keep[0], KB)
    position_abs = lax.axis_index("blk") * block_rows + jnp.arange(block_rows, dtype=jnp.int32)
    live_keys = ((keep_rows > 0) & (position_abs < prompt_lengths[0])).astype(jnp.int32)[None, :]
    piece_kv = lax.all_gather(prompt_kv, "blk", axis=1, tiled=True)
    blk_count = lax.axis_size("blk")
    page_count = block_rows // PAGE
    packed = jnp.concatenate([live_keys[0], page_owner[0, :, 0]])
    packed_all = lax.all_gather(packed, "blk", axis=0, tiled=True).reshape(blk_count, -1)
    piece_live = packed_all[:, :block_rows].reshape(1, -1)
    owners_all = packed_all[:, block_rows:]
    count = piece_kv.shape[1]
    key_heads = piece_kv[0, :, :kv_width].reshape(count, KVH, HD)
    value_heads = piece_kv[0, :, kv_width:].reshape(count, KVH, HD)
    visible = (piece_live[0] > 0)[None, None, None, :]
    running_max, denom, numerator = absorb(
        carry_state, query_heads, key_heads, value_heads, visible
    )
    attended = (numerator / denom[..., None]).reshape(tok_rows, H * HD).astype(jnp.bfloat16)
    projected = jnp.dot(
        attended,
        gather_rows(out_weight, "exp"),
        preferred_element_type=jnp.float32,
    )
    stream = (residual[0].astype(jnp.float32) + projected).astype(jnp.bfloat16)
    stream_f32 = stream.astype(jnp.float32)
    normed = (
        stream_f32 * lax.rsqrt(jnp.mean(stream_f32 * stream_f32, axis=-1, keepdims=True) + EPSILON)
    ).astype(jnp.bfloat16)
    exp_count = lax.axis_size("exp")
    experts = EXP_DEV * exp_count
    capacity = min(tok_rows, 5 * tok_rows * TOPK // (4 * experts))
    flat_routes = routes[0].reshape(-1)
    slot_index = flat_routes * capacity + rank_within(flat_routes, experts)
    slot_iota = jnp.arange(experts * capacity, dtype=jnp.int32)
    token_slots = slot_index.reshape(tok_rows, TOPK)
    hits = token_slots[None, :, :] == slot_iota[:, None, None]
    placer = jnp.any(hits, axis=-1).astype(jnp.bfloat16)
    dispatch = jnp.dot(placer, normed, preferred_element_type=jnp.float32).astype(jnp.bfloat16)
    dispatch = dispatch.reshape(experts, capacity, D)
    arrived = lax.all_to_all(dispatch, "exp", split_axis=0, concat_axis=0, tiled=True)
    count = arrived.shape[1]
    grouped = arrived.reshape(exp_count, EXP_DEV, count, D)
    picked_rows = grouped[:, 0].reshape(exp_count * count, D)
    gate_up = jnp.dot(picked_rows, gate_up_weight[0], preferred_element_type=jnp.float32)
    hidden = (jax.nn.silu(gate_up[:, :FF]) * gate_up[:, FF:]).astype(jnp.bfloat16)
    result = jnp.dot(hidden, down_weight[0], preferred_element_type=jnp.float32).astype(
        jnp.bfloat16
    )
    results = [result.reshape(exp_count, count, D)]
    outgoing = jnp.stack(results, axis=1).reshape(exp_count * EXP_DEV, count, D)
    returned = lax.all_to_all(outgoing, "exp", split_axis=0, concat_axis=0, tiled=True)
    slot_weight = jnp.sum(
        jnp.where(
            token_slots[:, :, None] == slot_iota[None, None, :],
            route_weight[0][:, :, None],
            0.0,
        ),
        axis=1,
    )
    weight_hi = slot_weight.astype(jnp.bfloat16)
    weight_lo = (slot_weight - weight_hi.astype(jnp.float32)).astype(jnp.bfloat16)
    returned_rows = returned.reshape(experts * capacity, D)
    combined = jnp.dot(weight_hi, returned_rows, preferred_element_type=jnp.float32) + jnp.dot(
        weight_lo, returned_rows, preferred_element_type=jnp.float32
    )
    layer_out = (stream_f32 + combined).astype(jnp.bfloat16)
    page_capacity = max(2, 2 * page_count // blk_count)
    me = lax.axis_index("blk")
    page_rank = jax.vmap(lambda labels: rank_within(labels, blk_count))(owners_all)
    block_of = jnp.arange(blk_count, dtype=jnp.int32)[:, None]
    page_slot = jnp.where(owners_all == me, block_of * page_capacity + page_rank, -1).reshape(-1)
    out_rows = blk_count * page_capacity * PAGE
    row_slot = jnp.arange(out_rows, dtype=jnp.int32) // PAGE
    prompt_rows = piece_kv.shape[1]
    src_page = jnp.arange(prompt_rows, dtype=jnp.int32) // PAGE
    same_row = (jnp.arange(out_rows)[:, None] % PAGE) == (jnp.arange(prompt_rows)[None, :] % PAGE)
    chooser = (page_slot[src_page][None, :] == row_slot[:, None]) & same_row
    cache_pages = jnp.dot(
        chooser.astype(jnp.bfloat16), piece_kv[0], preferred_element_type=jnp.float32
    ).astype(jnp.bfloat16)[None]
    return (attended[None], layer_out[None], cache_pages)


def solution(mesh):
    return jax.shard_map(
        local,
        mesh=mesh,
        in_specs=(
            P("exp", "blk", None),
            P("exp", "blk", None),
            P("exp", "blk", None),
            P("exp", "blk", None),
            P("exp"),
            P("exp", "blk"),
            P("exp", "blk", None),
            P("exp", None),
            P("exp", "blk", None),
            P("exp", "blk", None),
            P("exp", None, None),
            P("exp", None, None),
            P("exp", "blk", None),
        ),
        out_specs=(P("exp", "blk", None), P("exp", "blk", None), P("exp", "blk", None)),
        check_vma=False,
    )
```

```python
import jax
import jax.numpy as jnp
from jax import lax
from jax.sharding import PartitionSpec as P
from jax.experimental import pallas as pl

D = 1024
H = 16
KVH = 8
HD = 64
FF = 512
TOPK = 8
EXP_DEV = 1
KB = 32
PAGE = 8


SCALE = 0.125
NEGATIVE = -1e30
EPSILON = 1e-06


def segment_of(lengths, count):
    ends = jnp.cumsum(lengths)
    position = jnp.arange(count, dtype=jnp.int32)
    return jnp.sum((position[:, None] >= ends[None, :]).astype(jnp.int32), axis=1)


def rank_within(labels, count):
    onehot = (labels[:, None] == jnp.arange(count, dtype=jnp.int32)[None, :]).astype(jnp.int32)
    before = jnp.cumsum(onehot, axis=0) - onehot
    return jnp.sum(before * onehot, axis=1)


def gather_rows(piece, axis):
    count = lax.axis_size(axis)
    tiles = jnp.broadcast_to(piece[None], (count,) + piece.shape)
    whole = lax.all_to_all(tiles, axis, split_axis=0, concat_axis=0, tiled=True)
    return whole.reshape((count * piece.shape[0],) + piece.shape[1:])


def prompt_attend_kernel(q_ref, kv_ref, live_ref, m_ref, l_ref, acc_ref, out_ref):
    kv_width = KVH * HD
    visible = live_ref[...] > 0
    for h in range(H):
        k = h // (H // KVH)
        qh = q_ref[:, h * HD:(h + 1) * HD]
        kh = kv_ref[:, k * HD:(k + 1) * HD]
        vh = kv_ref[:, kv_width + k * HD:kv_width + (k + 1) * HD]
        s = lax.dot_general(qh, kh, (((1,), (1,)), ((), ())), preferred_element_type=jnp.float32) * SCALE
        m_old = m_ref[:, h:h + 1]
        m_new = jnp.maximum(m_old, jnp.max(jnp.where(visible, s, NEGATIVE), axis=1, keepdims=True))
        factor = jnp.exp(m_old - m_new)
        w = jnp.where(visible, jnp.exp(s - m_new), 0.0)
        l_new = l_ref[:, h:h + 1] * factor + jnp.sum(w, axis=1, keepdims=True)
        added = jnp.dot(w.astype(jnp.bfloat16), vh, preferred_element_type=jnp.float32)
        acc = acc_ref[:, h * HD:(h + 1) * HD] * factor + added
        out_ref[:, h * HD:(h + 1) * HD] = (acc / l_new).astype(jnp.bfloat16)


def prompt_attend(q, kv, live, m0, l0, acc0):
    tok = q.shape[0]
    return pl.pallas_call(
        prompt_attend_kernel,
        out_shape=jax.ShapeDtypeStruct((tok, H * HD), jnp.bfloat16),
    )(q, kv, live, m0, l0, acc0)


def absorb(carry_state, query_heads, key_heads, value_heads, visible):
    running_max, denom, numerator = carry_state
    scores = (
        jnp.einsum("tkgd,skd->tkgs", query_heads, key_heads, preferred_element_type=jnp.float32)
        * SCALE
    )
    new_max = jnp.maximum(running_max, jnp.max(jnp.where(visible, scores, NEGATIVE), axis=-1))
    factor = jnp.exp(running_max - new_max)
    weight = jnp.where(visible, jnp.exp(scores - new_max[..., None]), 0.0)
    denom = denom * factor + jnp.sum(weight, axis=-1)
    added = jnp.einsum(
        "tkgs,skd->tkgd",
        weight.astype(jnp.bfloat16),
        value_heads,
        preferred_element_type=jnp.float32,
    )
    numerator = numerator * factor[..., None] + added
    return (new_max, denom, numerator)


def local(
    residual,
    queries,
    suffix_kv,
    prompt_kv,
    prompt_lengths,
    block_keep,
    suffix_lengths,
    out_weight,
    routes,
    route_weight,
    gate_up_weight,
    down_weight,
    page_owner,
):
    tok_rows = queries.shape[1]
    kv_width = suffix_kv.shape[2] // 2
    group_size = H // KVH
    query_heads = queries[0].reshape(tok_rows, KVH, group_size, HD)
    own_keys = suffix_kv[0, :, :kv_width].reshape(tok_rows, KVH, HD)
    own_values = suffix_kv[0, :, kv_width:].reshape(tok_rows, KVH, HD)
    segment = segment_of(suffix_lengths[0, 0], tok_rows)
    position = jnp.arange(tok_rows, dtype=jnp.int32)
    own_seen = ((segment[:, None] == segment[None, :]) & (position[None, :] <= position[:, None]))[
        :, None, None, :
    ]
    start_state = (
        jnp.full((tok_rows, KVH, group_size), NEGATIVE, jnp.float32),
        jnp.zeros((tok_rows, KVH, group_size), jnp.float32),
        jnp.zeros((tok_rows, KVH, group_size, HD), jnp.float32),
    )
    carry_state = absorb(start_state, query_heads, own_keys, own_values, own_seen)
    block_rows = prompt_kv.shape[1]
    keep_rows = jnp.repeat(block_keep[0], KB)
    position_abs = lax.axis_index("blk") * block_rows + jnp.arange(block_rows, dtype=jnp.int32)
    live_keys = ((keep_rows > 0) & (position_abs < prompt_lengths[0])).astype(jnp.int32)[None, :]
    piece_kv = lax.all_gather(prompt_kv, "blk", axis=1, tiled=True)
    blk_count = lax.axis_size("blk")
    page_count = block_rows // PAGE
    packed = jnp.concatenate([live_keys[0], page_owner[0, :, 0]])
    packed_all = lax.all_gather(packed, "blk", axis=0, tiled=True).reshape(blk_count, -1)
    piece_live = packed_all[:, :block_rows].reshape(1, -1)
    owners_all = packed_all[:, block_rows:]
    suffix_max, suffix_denom, suffix_numerator = carry_state
    attended = prompt_attend(
        queries[0],
        piece_kv[0],
        piece_live,
        suffix_max.reshape(tok_rows, H),
        suffix_denom.reshape(tok_rows, H),
        suffix_numerator.reshape(tok_rows, H * HD),
    )
    projected = jnp.dot(
        attended,
        gather_rows(out_weight, "exp"),
        preferred_element_type=jnp.float32,
    )
    stream = (residual[0].astype(jnp.float32) + projected).astype(jnp.bfloat16)
    stream_f32 = stream.astype(jnp.float32)
    normed = (
        stream_f32 * lax.rsqrt(jnp.mean(stream_f32 * stream_f32, axis=-1, keepdims=True) + EPSILON)
    ).astype(jnp.bfloat16)
    exp_count = lax.axis_size("exp")
    experts = EXP_DEV * exp_count
    capacity = min(tok_rows, 5 * tok_rows * TOPK // (4 * experts))
    flat_routes = routes[0].reshape(-1)
    slot_index = flat_routes * capacity + rank_within(flat_routes, experts)
    slot_iota = jnp.arange(experts * capacity, dtype=jnp.int32)
    token_slots = slot_index.reshape(tok_rows, TOPK)
    hits = token_slots[None, :, :] == slot_iota[:, None, None]
    placer = jnp.any(hits, axis=-1).astype(jnp.bfloat16)
    dispatch = jnp.dot(placer, normed, preferred_element_type=jnp.float32).astype(jnp.bfloat16)
    dispatch = dispatch.reshape(experts, capacity, D)
    arrived = lax.all_to_all(dispatch, "exp", split_axis=0, concat_axis=0, tiled=True)
    count = arrived.shape[1]
    grouped = arrived.reshape(exp_count, EXP_DEV, count, D)
    picked_rows = grouped[:, 0].reshape(exp_count * count, D)
    gate_up = jnp.dot(picked_rows, gate_up_weight[0], preferred_element_type=jnp.float32)
    hidden = (jax.nn.silu(gate_up[:, :FF]) * gate_up[:, FF:]).astype(jnp.bfloat16)
    result = jnp.dot(hidden, down_weight[0], preferred_element_type=jnp.float32).astype(
        jnp.bfloat16
    )
    results = [result.reshape(exp_count, count, D)]
    outgoing = jnp.stack(results, axis=1).reshape(exp_count * EXP_DEV, count, D)
    returned = lax.all_to_all(outgoing, "exp", split_axis=0, concat_axis=0, tiled=True)
    slot_weight = jnp.sum(
        jnp.where(
            token_slots[:, :, None] == slot_iota[None, None, :],
            route_weight[0][:, :, None],
            0.0,
        ),
        axis=1,
    )
    combined = jnp.dot(
        slot_weight,
        returned.reshape(experts * capacity, D).astype(jnp.float32),
        precision=lax.Precision.HIGHEST,
        preferred_element_type=jnp.float32,
    )
    layer_out = (stream_f32 + combined).astype(jnp.bfloat16)
    page_capacity = max(2, 2 * page_count // blk_count)
    me = lax.axis_index("blk")
    page_rank = jax.vmap(lambda labels: rank_within(labels, blk_count))(owners_all)
    block_of = jnp.arange(blk_count, dtype=jnp.int32)[:, None]
    page_slot = jnp.where(owners_all == me, block_of * page_capacity + page_rank, -1).reshape(-1)
    out_rows = blk_count * page_capacity * PAGE
    row_slot = jnp.arange(out_rows, dtype=jnp.int32) // PAGE
    prompt_rows = piece_kv.shape[1]
    src_page = jnp.arange(prompt_rows, dtype=jnp.int32) // PAGE
    same_row = (jnp.arange(out_rows)[:, None] % PAGE) == (jnp.arange(prompt_rows)[None, :] % PAGE)
    chooser = (page_slot[src_page][None, :] == row_slot[:, None]) & same_row
    cache_pages = jnp.dot(
        chooser.astype(jnp.bfloat16), piece_kv[0], preferred_element_type=jnp.float32
    ).astype(jnp.bfloat16)[None]
    return (attended[None], layer_out[None], cache_pages)


def solution(mesh):
    return jax.shard_map(
        local,
        mesh=mesh,
        in_specs=(
            P("exp", "blk", None),
            P("exp", "blk", None),
            P("exp", "blk", None),
            P("exp", "blk", None),
            P("exp"),
            P("exp", "blk"),
            P("exp", "blk", None),
            P("exp", None),
            P("exp", "blk", None),
            P("exp", "blk", None),
            P("exp", None, None),
            P("exp", None, None),
            P("exp", "blk", None),
        ),
        out_specs=(P("exp", "blk", None), P("exp", "blk", None), P("exp", "blk", None)),
        check_vma=False,
    )
```

```python
import jax
import jax.numpy as jnp
from jax import lax
from jax.sharding import PartitionSpec as P

D = 1024
H = 16
KVH = 8
HD = 64
FF = 512
TOPK = 8
EXP_DEV = 1
KB = 32
PAGE = 8


SCALE = 0.125
NEGATIVE = -1e30
EPSILON = 1e-06


def segment_of(lengths, count):
    ends = jnp.cumsum(lengths)
    position = jnp.arange(count, dtype=jnp.int32)
    return jnp.sum((position[:, None] >= ends[None, :]).astype(jnp.int32), axis=1)


def rank_within(labels, count):
    onehot = (labels[:, None] == jnp.arange(count, dtype=jnp.int32)[None, :]).astype(jnp.int32)
    before = jnp.cumsum(onehot, axis=0) - onehot
    return jnp.sum(before * onehot, axis=1)


def gather_rows(piece, axis):
    count = lax.axis_size(axis)
    tiles = jnp.broadcast_to(piece[None], (count,) + piece.shape)
    whole = lax.all_to_all(tiles, axis, split_axis=0, concat_axis=0, tiled=True)
    return whole.reshape((count * piece.shape[0],) + piece.shape[1:])


def absorb_blocks(carry_state, query_heads, keys_b, values_b, visible):
    running_max, denom, numerator = carry_state
    scores = (
        jnp.einsum("tkgd,nkds->tkgns", query_heads, keys_b, preferred_element_type=jnp.float32)
        * SCALE
    )
    masked = jnp.where(visible, scores, NEGATIVE)
    new_max = jnp.maximum(running_max, jnp.max(masked, axis=(-2, -1)))
    factor = jnp.exp(running_max - new_max)
    weight = jnp.where(visible, jnp.exp(scores - new_max[..., None, None]), 0.0)
    denom = denom * factor + jnp.sum(weight, axis=(-2, -1))
    added = jnp.einsum(
        "tkgns,nkds->tkgd",
        weight.astype(jnp.bfloat16),
        values_b,
        preferred_element_type=jnp.float32,
    )
    numerator = numerator * factor[..., None] + added
    return (new_max, denom, numerator)


def absorb(carry_state, query_heads, key_heads, value_heads, visible):
    running_max, denom, numerator = carry_state
    scores = (
        jnp.einsum("tkgd,skd->tkgs", query_heads, key_heads, preferred_element_type=jnp.float32)
        * SCALE
    )
    new_max = jnp.maximum(running_max, jnp.max(jnp.where(visible, scores, NEGATIVE), axis=-1))
    factor = jnp.exp(running_max - new_max)
    weight = jnp.where(visible, jnp.exp(scores - new_max[..., None]), 0.0)
    denom = denom * factor + jnp.sum(weight, axis=-1)
    added = jnp.einsum(
        "tkgs,skd->tkgd",
        weight.astype(jnp.bfloat16),
        value_heads,
        preferred_element_type=jnp.float32,
    )
    numerator = numerator * factor[..., None] + added
    return (new_max, denom, numerator)


def local(
    residual,
    queries,
    suffix_kv,
    prompt_kv,
    prompt_lengths,
    block_keep,
    suffix_lengths,
    out_weight,
    routes,
    route_weight,
    gate_up_weight,
    down_weight,
    page_owner,
):
    tok_rows = queries.shape[1]
    kv_width = suffix_kv.shape[2] // 2
    group_size = H // KVH
    query_heads = queries[0].reshape(tok_rows, KVH, group_size, HD)
    own_keys = suffix_kv[0, :, :kv_width].reshape(tok_rows, KVH, HD)
    own_values = suffix_kv[0, :, kv_width:].reshape(tok_rows, KVH, HD)
    segment = segment_of(suffix_lengths[0, 0], tok_rows)
    position = jnp.arange(tok_rows, dtype=jnp.int32)
    own_seen = ((segment[:, None] == segment[None, :]) & (position[None, :] <= position[:, None]))[
        :, None, None, :
    ]
    start_state = (
        jnp.full((tok_rows, KVH, group_size), NEGATIVE, jnp.float32),
        jnp.zeros((tok_rows, KVH, group_size), jnp.float32),
        jnp.zeros((tok_rows, KVH, group_size, HD), jnp.float32),
    )
    carry_state = absorb(start_state, query_heads, own_keys, own_values, own_seen)
    block_rows = prompt_kv.shape[1]
    keep_rows = jnp.repeat(block_keep[0], KB)
    position_abs = lax.axis_index("blk") * block_rows + jnp.arange(block_rows, dtype=jnp.int32)
    live_keys = ((keep_rows > 0) & (position_abs < prompt_lengths[0])).astype(jnp.int32)[None, :]
    local_t = prompt_kv[0].T.reshape(2, KVH, HD, block_rows)
    blocks = lax.all_gather(local_t, "blk", axis=0, tiled=False)
    blk_count = lax.axis_size("blk")
    page_count = block_rows // PAGE
    packed = jnp.concatenate([live_keys[0], page_owner[0, :, 0]])
    packed_all = lax.all_gather(packed, "blk", axis=0, tiled=True).reshape(blk_count, -1)
    piece_live = packed_all[:, :block_rows].reshape(1, -1)
    owners_all = packed_all[:, block_rows:]
    visible = (piece_live[0] > 0).reshape(blk_count, block_rows)[None, None, None]
    running_max, denom, numerator = absorb_blocks(
        carry_state, query_heads, blocks[:, 0], blocks[:, 1], visible
    )
    attended = (numerator / denom[..., None]).reshape(tok_rows, H * HD).astype(jnp.bfloat16)
    projected = jnp.dot(
        attended,
        gather_rows(out_weight, "exp"),
        preferred_element_type=jnp.float32,
    )
    stream = (residual[0].astype(jnp.float32) + projected).astype(jnp.bfloat16)
    stream_f32 = stream.astype(jnp.float32)
    normed = (
        stream_f32 * lax.rsqrt(jnp.mean(stream_f32 * stream_f32, axis=-1, keepdims=True) + EPSILON)
    ).astype(jnp.bfloat16)
    exp_count = lax.axis_size("exp")
    experts = EXP_DEV * exp_count
    capacity = min(tok_rows, 5 * tok_rows * TOPK // (4 * experts))
    flat_routes = routes[0].reshape(-1)
    slot_index = flat_routes * capacity + rank_within(flat_routes, experts)
    slot_iota = jnp.arange(experts * capacity, dtype=jnp.int32)
    token_slots = slot_index.reshape(tok_rows, TOPK)
    hits = token_slots[None, :, :] == slot_iota[:, None, None]
    placer = jnp.any(hits, axis=-1).astype(jnp.bfloat16)
    dispatch = jnp.dot(placer, normed, preferred_element_type=jnp.float32).astype(jnp.bfloat16)
    dispatch = dispatch.reshape(experts, capacity, D)
    arrived = lax.all_to_all(dispatch, "exp", split_axis=0, concat_axis=0, tiled=True)
    count = arrived.shape[1]
    grouped = arrived.reshape(exp_count, EXP_DEV, count, D)
    picked_rows = grouped[:, 0].reshape(exp_count * count, D)
    gate_up = jnp.dot(picked_rows, gate_up_weight[0], preferred_element_type=jnp.float32)
    hidden = (jax.nn.silu(gate_up[:, :FF]) * gate_up[:, FF:]).astype(jnp.bfloat16)
    result = jnp.dot(hidden, down_weight[0], preferred_element_type=jnp.float32).astype(
        jnp.bfloat16
    )
    results = [result.reshape(exp_count, count, D)]
    outgoing = jnp.stack(results, axis=1).reshape(exp_count * EXP_DEV, count, D)
    returned = lax.all_to_all(outgoing, "exp", split_axis=0, concat_axis=0, tiled=True)
    slot_weight = jnp.sum(
        jnp.where(
            token_slots[:, :, None] == slot_iota[None, None, :],
            route_weight[0][:, :, None],
            0.0,
        ),
        axis=1,
    )
    combined = jnp.dot(
        slot_weight,
        returned.reshape(experts * capacity, D).astype(jnp.float32),
        precision=lax.Precision.HIGHEST,
        preferred_element_type=jnp.float32,
    )
    layer_out = (stream_f32 + combined).astype(jnp.bfloat16)
    page_capacity = max(2, 2 * page_count // blk_count)
    me = lax.axis_index("blk")
    page_rank = jax.vmap(lambda labels: rank_within(labels, blk_count))(owners_all)
    block_of = jnp.arange(blk_count, dtype=jnp.int32)[:, None]
    page_slot = jnp.where(owners_all == me, block_of * page_capacity + page_rank, -1).reshape(-1)
    out_rows = blk_count * page_capacity * PAGE
    row_slot = jnp.arange(out_rows, dtype=jnp.int32) // PAGE
    prompt_rows = blk_count * block_rows
    src_page = jnp.arange(prompt_rows, dtype=jnp.int32) // PAGE
    same_row = (jnp.arange(out_rows)[:, None] % PAGE) == (jnp.arange(prompt_rows)[None, :] % PAGE)
    chooser = (page_slot[src_page][None, :] == row_slot[:, None]) & same_row
    prompt_full = jnp.transpose(blocks, (0, 4, 1, 2, 3)).reshape(prompt_rows, -1)
    cache_pages = jnp.dot(
        chooser.astype(jnp.bfloat16), prompt_full, preferred_element_type=jnp.float32
    ).astype(jnp.bfloat16)[None]
    return (attended[None], layer_out[None], cache_pages)


def solution(mesh):
    return jax.shard_map(
        local,
        mesh=mesh,
        in_specs=(
            P("exp", "blk", None),
            P("exp", "blk", None),
            P("exp", "blk", None),
            P("exp", "blk", None),
            P("exp"),
            P("exp", "blk"),
            P("exp", "blk", None),
            P("exp", None),
            P("exp", "blk", None),
            P("exp", "blk", None),
            P("exp", None, None),
            P("exp", None, None),
            P("exp", "blk", None),
        ),
        out_specs=(P("exp", "blk", None), P("exp", "blk", None), P("exp", "blk", None)),
        check_vma=False,
    )
```

```python
import jax
import jax.numpy as jnp
from jax import lax
from jax.sharding import PartitionSpec as P

D = 1024
H = 16
KVH = 8
HD = 64
FF = 512
TOPK = 8
EXP_DEV = 1
KB = 32
PAGE = 8


SCALE = 0.125
NEGATIVE = -1e30
EPSILON = 1e-06


def segment_of(lengths, count):
    ends = jnp.cumsum(lengths)
    position = jnp.arange(count, dtype=jnp.int32)
    return jnp.sum((position[:, None] >= ends[None, :]).astype(jnp.int32), axis=1)


def rank_within(labels, count):
    onehot = (labels[:, None] == jnp.arange(count, dtype=jnp.int32)[None, :]).astype(jnp.int32)
    before = jnp.cumsum(onehot, axis=0) - onehot
    return jnp.sum(before * onehot, axis=1)


def gather_rows(piece, axis):
    count = lax.axis_size(axis)
    tiles = jnp.broadcast_to(piece[None], (count,) + piece.shape)
    whole = lax.all_to_all(tiles, axis, split_axis=0, concat_axis=0, tiled=True)
    return whole.reshape((count * piece.shape[0],) + piece.shape[1:])


def absorb(carry_state, query_heads, key_heads, value_heads, visible):
    running_max, denom, numerator = carry_state
    scores = (
        jnp.einsum("tkgd,skd->tkgs", query_heads, key_heads, preferred_element_type=jnp.float32)
        * SCALE
    )
    new_max = jnp.maximum(running_max, jnp.max(jnp.where(visible, scores, NEGATIVE), axis=-1))
    factor = jnp.exp(running_max - new_max)
    weight = jnp.where(visible, jnp.exp(scores - new_max[..., None]), 0.0)
    denom = denom * factor + jnp.sum(weight, axis=-1)
    added = jnp.einsum(
        "tkgs,skd->tkgd",
        weight.astype(jnp.bfloat16),
        value_heads,
        preferred_element_type=jnp.float32,
    )
    numerator = numerator * factor[..., None] + added
    return (new_max, denom, numerator)


def local(
    residual,
    queries,
    suffix_kv,
    prompt_kv,
    prompt_lengths,
    block_keep,
    suffix_lengths,
    out_weight,
    routes,
    route_weight,
    gate_up_weight,
    down_weight,
    page_owner,
):
    tok_rows = queries.shape[1]
    kv_width = suffix_kv.shape[2] // 2
    group_size = H // KVH
    query_heads = queries[0].reshape(tok_rows, KVH, group_size, HD)
    own_keys = suffix_kv[0, :, :kv_width].reshape(tok_rows, KVH, HD)
    own_values = suffix_kv[0, :, kv_width:].reshape(tok_rows, KVH, HD)
    segment = segment_of(suffix_lengths[0, 0], tok_rows)
    position = jnp.arange(tok_rows, dtype=jnp.int32)
    own_seen = ((segment[:, None] == segment[None, :]) & (position[None, :] <= position[:, None]))[
        :, None, None, :
    ]
    start_state = (
        jnp.full((tok_rows, KVH, group_size), NEGATIVE, jnp.float32),
        jnp.zeros((tok_rows, KVH, group_size), jnp.float32),
        jnp.zeros((tok_rows, KVH, group_size, HD), jnp.float32),
    )
    carry_state = absorb(start_state, query_heads, own_keys, own_values, own_seen)
    block_rows = prompt_kv.shape[1]
    keep_rows = jnp.repeat(block_keep[0], KB)
    position_abs = lax.axis_index("blk") * block_rows + jnp.arange(block_rows, dtype=jnp.int32)
    live_keys = ((keep_rows > 0) & (position_abs < prompt_lengths[0])).astype(jnp.int32)[None, :]
    piece_kv = lax.all_gather(prompt_kv, "blk", axis=1, tiled=True)
    blk_count = lax.axis_size("blk")
    page_count = block_rows // PAGE
    packed = jnp.concatenate([live_keys[0], page_owner[0, :, 0]])
    packed_all = lax.all_gather(packed, "blk", axis=0, tiled=True).reshape(blk_count, -1)
    piece_live = packed_all[:, :block_rows].reshape(1, -1)
    owners_all = packed_all[:, block_rows:]
    count = piece_kv.shape[1]
    key_heads = piece_kv[0, :, :kv_width].reshape(count, KVH, HD)
    value_heads = piece_kv[0, :, kv_width:].reshape(count, KVH, HD)
    visible = (piece_live[0] > 0)[None, None, None, :]
    running_max, denom, numerator = absorb(
        carry_state, query_heads, key_heads, value_heads, visible
    )
    attended = (numerator / denom[..., None]).reshape(tok_rows, H * HD).astype(jnp.bfloat16)
    projected = jnp.dot(
        attended,
        gather_rows(out_weight, "exp"),
        preferred_element_type=jnp.float32,
    )
    stream = (residual[0].astype(jnp.float32) + projected).astype(jnp.bfloat16)
    stream_f32 = stream.astype(jnp.float32)
    normed = (
        stream_f32 * lax.rsqrt(jnp.mean(stream_f32 * stream_f32, axis=-1, keepdims=True) + EPSILON)
    ).astype(jnp.bfloat16)
    exp_count = lax.axis_size("exp")
    experts = EXP_DEV * exp_count
    capacity = min(tok_rows, 5 * tok_rows * TOPK // (4 * experts))
    flat_routes = routes[0].reshape(-1)
    slot_index = flat_routes * capacity + rank_within(flat_routes, experts)
    slot_iota = jnp.arange(experts * capacity, dtype=jnp.int32)
    token_slots = slot_index.reshape(tok_rows, TOPK)
    hits = token_slots[None, :, :] == slot_iota[:, None, None]
    placer = jnp.any(hits, axis=-1).astype(jnp.bfloat16)
    dispatch = jnp.dot(placer, normed, preferred_element_type=jnp.float32).astype(jnp.bfloat16)
    dispatch = dispatch.reshape(experts, capacity, D)
    arrived = lax.all_to_all(dispatch, "exp", split_axis=0, concat_axis=0, tiled=True)
    count = arrived.shape[1]
    grouped = arrived.reshape(exp_count, EXP_DEV, count, D)
    picked_rows = grouped[:, 0].reshape(exp_count * count, D)
    gate_up = jnp.dot(picked_rows, gate_up_weight[0], preferred_element_type=jnp.float32)
    hidden = (jax.nn.silu(gate_up[:, :FF]) * gate_up[:, FF:]).astype(jnp.bfloat16)
    result = jnp.dot(hidden, down_weight[0], preferred_element_type=jnp.float32).astype(
        jnp.bfloat16
    )
    results = [result.reshape(exp_count, count, D)]
    outgoing = jnp.stack(results, axis=1).reshape(exp_count * EXP_DEV, count, D)
    returned = lax.all_to_all(outgoing, "exp", split_axis=0, concat_axis=0, tiled=True)
    slot_weight = jnp.sum(
        jnp.where(
            token_slots[:, :, None] == slot_iota[None, None, :],
            route_weight[0][:, :, None],
            0.0,
        ),
        axis=1,
    )
    combined = jnp.dot(
        slot_weight,
        returned.reshape(experts * capacity, D).astype(jnp.float32),
        precision=lax.Precision.HIGH,
        preferred_element_type=jnp.float32,
    )
    layer_out = (stream_f32 + combined).astype(jnp.bfloat16)
    page_capacity = max(2, 2 * page_count // blk_count)
    me = lax.axis_index("blk")
    page_rank = jax.vmap(lambda labels: rank_within(labels, blk_count))(owners_all)
    block_of = jnp.arange(blk_count, dtype=jnp.int32)[:, None]
    page_slot = jnp.where(owners_all == me, block_of * page_capacity + page_rank, -1).reshape(-1)
    out_rows = blk_count * page_capacity * PAGE
    row_slot = jnp.arange(out_rows, dtype=jnp.int32) // PAGE
    prompt_rows = piece_kv.shape[1]
    src_page = jnp.arange(prompt_rows, dtype=jnp.int32) // PAGE
    same_row = (jnp.arange(out_rows)[:, None] % PAGE) == (jnp.arange(prompt_rows)[None, :] % PAGE)
    chooser = (page_slot[src_page][None, :] == row_slot[:, None]) & same_row
    cache_pages = jnp.dot(
        chooser.astype(jnp.bfloat16), piece_kv[0], preferred_element_type=jnp.float32
    ).astype(jnp.bfloat16)[None]
    return (attended[None], layer_out[None], cache_pages)


def solution(mesh):
    return jax.shard_map(
        local,
        mesh=mesh,
        in_specs=(
            P("exp", "blk", None),
            P("exp", "blk", None),
            P("exp", "blk", None),
            P("exp", "blk", None),
            P("exp"),
            P("exp", "blk"),
            P("exp", "blk", None),
            P("exp", None),
            P("exp", "blk", None),
            P("exp", "blk", None),
            P("exp", None, None),
            P("exp", None, None),
            P("exp", "blk", None),
        ),
        out_specs=(P("exp", "blk", None), P("exp", "blk", None), P("exp", "blk", None)),
        check_vma=False,
    )
```
